32 devices in a mesh: ctx: 8 (over z, core), fsdp: 4 (over y, x).
Axes of the slice: x: 2, y: 2, z: 4, core: 2. Of those that a mesh axis runs over, the one named last changes fastest.
Arguments:
- layer_in: bfloat16 [4, 8, 2, 128, 1024], P(None, 'ctx', None, 'fsdp'), may hold values from -6 to 6
- out_grad: bfloat16 [4, 8, 2, 128, 1024], P(None, 'ctx', None, 'fsdp'), may hold values from -6 to 6
- block_pairs: int32 [4, 8], replicated, may hold values from 0 to 7, each once within a row
- attn_gain: bfloat16 [1024], P('fsdp'), may hold values from 0.099609375 to 1.8984375
- attn_shift: bfloat16 [1024], P('fsdp'), may hold values from -3 to 3
- qkv_weight: bfloat16 [1024, 3072], P('fsdp'), may hold values from -0.25 to 0.25
- query_bias: bfloat16 [1024], P('fsdp'), may hold values from -3 to 3
- value_bias: bfloat16 [1024], P('fsdp'), may hold values from -0.29882812 to 0.29882812
- out_weight: bfloat16 [1024, 1024], P('fsdp'), may hold values from -2 to 2
- out_bias: bfloat16 [1024], P('fsdp'), may hold values from -3 to 3
- mlp_gain: bfloat16 [1024], P('fsdp'), may hold values from 0.099609375 to 1.8984375
- mlp_shift: bfloat16 [1024], P('fsdp'), may hold values from -3 to 3
- fc_weight: bfloat16 [1024, 4096], P('fsdp'), may hold values from -0.1875 to 0.1875
- fc_bias: bfloat16 [4096], P('fsdp'), may hold values from -3 to 3
- proj_weight: bfloat16 [4096, 1024], P('fsdp'), may hold values from -0.09375 to 0.09375
- proj_bias: bfloat16 [1024], P('fsdp'), may hold values from -3 to 3
Outputs:
- layer_out: bfloat16 [4, 8, 2, 128, 1024], P(None, 'ctx', None, 'fsdp')
- in_grad: float32 [4, 8, 2, 128, 1024], P(None, 'ctx', None, 'fsdp')
- attn_gain_grad: float32 [1024], P('fsdp')
- attn_shift_grad: float32 [1024], P('fsdp')
- qkv_weight_grad: float32 [1024, 3072], P('fsdp')
- query_bias_grad: float32 [1024], P('fsdp')
- value_bias_grad: float32 [1024], P('fsdp')
- out_weight_grad: float32 [1024, 1024], P('fsdp')
- out_bias_grad: float32 [1024], P('fsdp')
- mlp_gain_grad: float32 [1024], P('fsdp')
- mlp_shift_grad: float32 [1024], P('fsdp')
- fc_weight_grad: float32 [1024, 4096], P('fsdp')
- fc_bias_grad: float32 [4096], P('fsdp')
- proj_weight_grad: float32 [4096, 1024], P('fsdp')
- proj_bias_grad: float32 [1024], P('fsdp')
The draws below stay inside these ranges and needn't reach their ends.
Inputs may be any that keep to these rules, and one draw needn't show every extreme that they name: `block_pairs`: each row is a permutation: every device of ctx holds exactly one block pair of every sequence.
All inputs are finite; a program needn't handle non-finite values.
Results may differ from the reference program's by a relative error of at most 0.023.
Values may be sent and summed in bfloat16 or wider, within the bound.
No kernel may reach another device: no remote copies, remote signals or barrier semaphores. Data moves between devices by JAX's collectives and lax.ppermute only.
A program may use at most 320 MiB of HBM per device.

```python
import jax
import jax.numpy as jnp
from jax import lax

D = 1024
H = 16
HD = 64
FF = 4096
SEQS = 4
BLK = 128
LEN = 2048
N_CTX = 8


def levels(stream_key, shape, split, least, high):
    def one(dim, shards_of):
        heights = jax.random.uniform(jax.random.fold_in(jax.random.fold_in(stream_key, 6), dim), (shards_of,), jnp.float32, least / len(split), high / len(split))
        return jnp.repeat(jnp.exp(heights), shape[dim] // shards_of).reshape((-1,) + (1,) * (len(shape) - dim - 1))

    level = one(*split[0])
    for cut in split[1:]:
        level = level * one(*cut)
    return level


def noise(rng, dims, scale, reach, split=(), held_as=jnp.bfloat16):
    values = scale * jax.random.normal(rng, dims, jnp.float32)
    if split:
        values = values * levels(rng, dims, split, -0.22, 0.18)
    return jnp.clip(values, -reach, reach).astype(held_as)


def setup_inputs(seed: int = 0) -> dict:
    key_of = jax.random.split(jax.random.key(seed), 17)
    return {
        "layer_in": noise(key_of[0], (SEQS, N_CTX, 2, BLK, D), 1.0, 6.0, ((1, 8), (3, 4))),
        "out_grad": noise(key_of[1], (SEQS, N_CTX, 2, BLK, D), 1.0, 6.0, ((1, 8), (3, 4))),
        "block_pairs": jax.vmap(lambda own: jax.random.permutation(own, N_CTX))(jax.random.split(key_of[2], SEQS)).reshape((SEQS, N_CTX)).astype(jnp.int32),
        "attn_gain": jnp.clip(1.0 + 0.18 * jax.random.normal(key_of[3], (D,), jnp.float32), 0.099609375, 1.8984375).astype(jnp.bfloat16),
        "attn_shift": noise(key_of[4], (D,), 0.5, 3.0, ((0, 4),)),
        "qkv_weight": noise(key_of[5], (D, 3 * D), (D // 2) ** -0.5, 0.25, ((0, 4),)),
        "query_bias": noise(key_of[6], (D,), 0.5, 3.0, ((0, 4),)),
        "value_bias": noise(key_of[7], (D,), 0.05, 0.29882812, ((0, 4),)),
        "out_weight": noise(key_of[8], (D, D), (max(1, 16 * D // LEN)) ** -0.5, 2.0, ((0, 4),)),
        "out_bias": noise(key_of[9], (D,), 0.5, 3.0, ((0, 4),)),
        "mlp_gain": jnp.clip(1.0 + 0.18 * jax.random.normal(key_of[10], (D,), jnp.float32), 0.099609375, 1.8984375).astype(jnp.bfloat16),
        "mlp_shift": noise(key_of[11], (D,), 0.5, 3.0, ((0, 4),)),
        "fc_weight": noise(key_of[12], (D, FF), D ** -0.5, 0.1875, ((0, 4),)),
        "fc_bias": noise(key_of[13], (FF,), 0.5, 3.0, ((0, 4),)),
        "proj_weight": noise(key_of[14], (FF, D), FF ** -0.5, 0.09375, ((0, 4),)),
        "proj_bias": noise(key_of[15], (D,), 0.5, 3.0, ((0, 4),)),
    }


norm_eps = 1e-05
highest = lax.Precision.HIGHEST

@jax.custom_vjp
def low(v):
    return lax.optimization_barrier(v.astype(jnp.bfloat16)).astype(jnp.float32)

@jax.custom_vjp
def low_back(v):
    return v

def low_keep(v):
    return (low(v), None)

def low_pass(kept, grad):
    return (grad,)

def back_keep(v):
    return (v, None)

def back_low(kept, grad):
    return (low(grad),)
low.defvjp(low_keep, low_pass)
low_back.defvjp(back_keep, back_low)

def layer_norm(values, gain, shift):
    average = lax.optimization_barrier(jnp.mean(values, axis=-1, keepdims=True))
    centred = values - average
    spread = lax.optimization_barrier(jnp.mean(centred * centred, axis=-1, keepdims=True))
    return centred * lax.rsqrt(spread + norm_eps) * gain + shift

def gelu_tanh(values):
    return jax.nn.gelu(values, approximate=True)

def product(left, right):
    return jnp.dot(left, right, precision=highest)

def attend_head(items):
    query, keys, values, places = items
    scores = low_back(jnp.dot(query, keys.T, precision=highest))
    allowed = places[None, :] <= places[:, None]
    scores = jnp.where(allowed, scores, -1e+30)
    row_peak = lax.optimization_barrier(jnp.max(scores, axis=1, keepdims=True))
    raised = jnp.exp(scores - row_peak)
    weights = raised / lax.optimization_barrier(jnp.sum(raised, axis=1, keepdims=True))
    return jnp.dot(low(weights), values, precision=highest)

def by_head(array):
    return array.reshape(SEQS, LEN, H, HD).transpose(0, 2, 1, 3).reshape(SEQS * H, LEN, HD)

def forward(inputs, attn_gain, attn_shift, qkv_weight, query_bias, value_bias, out_weight, out_bias, mlp_gain, mlp_shift, fc_weight, fc_bias, proj_weight, proj_bias, places):
    rows_all = inputs.reshape(-1, D)
    normed = low(layer_norm(rows_all, attn_gain, attn_shift))
    mixed = product(normed, qkv_weight)
    query = low_back(low((mixed[:, :D] + query_bias) * 0.125))
    keys = low_back(low(mixed[:, D:2 * D]))
    values = low_back(low(mixed[:, 2 * D:] + value_bias))
    head_places = jnp.repeat(places.reshape(SEQS, LEN), H, axis=0)
    attended = lax.map(jax.checkpoint(attend_head), (by_head(query), by_head(keys), by_head(values), head_places))
    attended = attended.reshape(SEQS, H, LEN, HD).transpose(0, 2, 1, 3).reshape(-1, D)
    attended = low_back(low(attended))
    branch = low_back(product(attended, out_weight) + out_bias)
    middle = rows_all + branch
    normed_mlp = low(layer_norm(middle, mlp_gain, mlp_shift))
    hidden = low_back(product(normed_mlp, fc_weight) + fc_bias)
    activated = low(gelu_tanh(hidden))
    return middle + product(activated, proj_weight) + proj_bias

def reference(layer_in, out_grad, block_pairs, attn_gain, attn_shift, qkv_weight, query_bias, value_bias, out_weight, out_bias, mlp_gain, mlp_shift, fc_weight, fc_bias, proj_weight, proj_bias):
    halves = jnp.stack([block_pairs, 2 * N_CTX - 1 - block_pairs], axis=2).astype(jnp.int32)
    places = halves[..., None] * BLK + jnp.arange(BLK, dtype=jnp.int32)
    arrays = tuple((array.astype(jnp.float32) for array in (layer_in, attn_gain, attn_shift, qkv_weight, query_bias, value_bias, out_weight, out_bias, mlp_gain, mlp_shift, fc_weight, fc_bias, proj_weight, proj_bias)))

    def wrapped(*params):
        return forward(*params, places)
    result, pullback = jax.vjp(wrapped, *arrays)
    grads = pullback(out_grad.reshape(-1, D).astype(jnp.float32))
    full_shape = layer_in.shape
    return (result.reshape(full_shape).astype(jnp.bfloat16), grads[0].reshape(full_shape), grads[1], grads[2], grads[3], grads[4], grads[5], grads[6], grads[7], grads[8], grads[9], grads[10], grads[11], grads[12], grads[13])
```

```python
import jax
import jax.numpy as jnp
from jax import lax
from jax.sharding import PartitionSpec as P

HD = 64


norm_eps = 1e-05
masked_score = -1e30


def for_sending(array):
    return jax.tree.map(lambda a: a.astype(jnp.bfloat16) if a.dtype == jnp.float32 else a, array)


def layer_norm(values, gain, shift):
    average = jnp.mean(values, axis=-1, keepdims=True)
    centred = values - average
    spread = jnp.mean(centred * centred, axis=-1, keepdims=True)
    return centred * lax.rsqrt(spread + norm_eps) * gain + shift


def gelu_tanh(values):
    return jax.nn.gelu(values, approximate=True)


def contract_last(left, right):
    return lax.dot_general(
        left, right, (((1,), (1,)), ((), ())), preferred_element_type=jnp.float32
    )


def contract_first(left, right):
    return lax.dot_general(
        left, right, (((0,), (0,)), ((), ())), preferred_element_type=jnp.float32
    )


def head_scores(query, keys, query_places, key_places):
    scores = contract_last(query, keys)
    return jnp.where(key_places[None, :] <= query_places[:, None], scores, masked_score)


def score_grads(query, keys, values, grad_out, summary, row_sum, query_places, key_places):
    scores = head_scores(query, keys, query_places, key_places)
    probs = jnp.exp(scores - summary[:, None])
    grad_probs = contract_last(grad_out, values)
    row_sum = jnp.sum(probs * grad_probs, axis=1)
    grad_scores = (probs * (grad_probs - row_sum[:, None])).astype(jnp.bfloat16)
    return (probs.astype(jnp.bfloat16), grad_scores, row_sum)


def attend_forward(items):
    query, keys, values, query_places, key_places = items
    outputs = []
    summaries = []
    for head_index in range(query.shape[1] // HD):
        columns = slice(head_index * HD, (head_index + 1) * HD)
        scores = head_scores(query[:, columns], keys[:, columns], query_places, key_places)
        row_peak = jnp.max(scores, axis=1, keepdims=True)
        raised = jnp.exp(scores - row_peak)
        row_total = jnp.sum(raised, axis=1, keepdims=True)
        weights = (raised / row_total).astype(jnp.bfloat16)
        outputs.append(
            jnp.dot(weights, values[:, columns], preferred_element_type=jnp.float32).astype(
                jnp.bfloat16
            )
        )
        summaries.append(row_peak[:, 0] + jnp.log(row_total[:, 0]))
    return (jnp.concatenate(outputs, axis=1), jnp.stack(summaries, axis=1))


def attend_backward(items):
    query, keys, values, grad_out, summary, query_places, key_places = items
    query_parts, key_parts, value_parts = ([], [], [])
    for head_index in range(query.shape[1] // HD):
        columns = slice(head_index * HD, (head_index + 1) * HD)
        probs_low, grad_scores, row_sum = score_grads(
            query[:, columns],
            keys[:, columns],
            values[:, columns],
            grad_out[:, columns],
            summary[:, head_index],
            None,
            query_places,
            key_places,
        )
        query_parts.append(
            jnp.dot(grad_scores, keys[:, columns], preferred_element_type=jnp.float32).astype(
                jnp.bfloat16
            )
        )
        key_parts.append(contract_first(grad_scores, query[:, columns]))
        value_parts.append(contract_first(probs_low, grad_out[:, columns]))
    return (
        jnp.concatenate(query_parts, axis=1),
        jnp.concatenate(key_parts, axis=1),
        jnp.concatenate(value_parts, axis=1),
    )


def shards(
    layer_in,
    out_grad,
    block_pairs,
    attn_gain,
    attn_shift,
    qkv_weight,
    query_bias,
    value_bias,
    out_weight,
    out_bias,
    mlp_gain,
    mlp_shift,
    fc_weight,
    fc_bias,
    proj_weight,
    proj_bias,
):
    fsdp_size = lax.axis_size("fsdp")
    ctx_size = lax.axis_size("ctx")
    seq_count = layer_in.shape[0]
    half_rows = layer_in.shape[3]
    model_width = layer_in.shape[4]
    block_len = half_rows * fsdp_size
    pair_len = 2 * block_len
    group_width = model_width // fsdp_size
    gathered = (
        lax.all_gather(qkv_weight, "fsdp", axis=0, tiled=True),
        lax.all_gather(out_weight, "fsdp", axis=0, tiled=True),
        lax.all_gather(fc_weight, "fsdp", axis=0, tiled=True),
        lax.all_gather(proj_weight, "fsdp", axis=0, tiled=True),
        lax.all_gather(attn_gain, "fsdp", axis=0, tiled=True),
        lax.all_gather(attn_shift, "fsdp", axis=0, tiled=True),
        lax.all_gather(query_bias, "fsdp", axis=0, tiled=True),
        lax.all_gather(value_bias, "fsdp", axis=0, tiled=True),
        lax.all_gather(out_bias, "fsdp", axis=0, tiled=True),
        lax.all_gather(mlp_gain, "fsdp", axis=0, tiled=True),
        lax.all_gather(mlp_shift, "fsdp", axis=0, tiled=True),
        lax.all_gather(fc_bias, "fsdp", axis=0, tiled=True),
        lax.all_gather(proj_bias, "fsdp", axis=0, tiled=True),
    )
    qkv_full, out_full, fc_full, proj_full = (gathered[0], gathered[1], gathered[2], gathered[3])
    vectors = [piece.astype(jnp.float32) for piece in gathered[4:]]
    (
        gain_attn,
        shift_attn,
        bias_query,
        bias_value,
        bias_out,
        gain_mlp,
        shift_mlp,
        bias_fc,
        bias_proj,
    ) = vectors
    halves = jnp.stack([block_pairs, 2 * ctx_size - 1 - block_pairs], axis=2)
    key_places = (halves[..., None] * block_len + jnp.arange(block_len, dtype=jnp.int32)).reshape(
        seq_count, ctx_size, pair_len
    )
    query_places = lax.dynamic_slice_in_dim(key_places, lax.axis_index("ctx"), 1, 1).reshape(
        seq_count, pair_len
    )
    key_places = key_places.reshape(seq_count, ctx_size * pair_len)
    inputs = layer_in.reshape(-1, model_width).astype(jnp.float32)
    normed, attn_norm_back = jax.vjp(layer_norm, inputs, gain_attn, shift_attn)
    normed_low = normed.astype(jnp.bfloat16)
    mixed = jnp.dot(normed_low, qkv_full, preferred_element_type=jnp.float32)
    query = ((mixed[:, :model_width] + bias_query) * 0.125).astype(jnp.bfloat16)
    keys = mixed[:, model_width : 2 * model_width].astype(jnp.bfloat16)
    values = (mixed[:, 2 * model_width :] + bias_value).astype(jnp.bfloat16)

    def to_groups(array):
        return array.reshape(seq_count, 2, half_rows, fsdp_size, group_width)

    def to_pairs(array):
        return array.reshape(seq_count, 2, block_len, 1, group_width)

    query_heads, key_heads, value_heads = (
        lax.all_to_all(to_groups(query), "fsdp", split_axis=3, concat_axis=2, tiled=True),
        lax.all_to_all(to_groups(keys), "fsdp", split_axis=3, concat_axis=2, tiled=True),
        lax.all_to_all(to_groups(values), "fsdp", split_axis=3, concat_axis=2, tiled=True),
    )
    query_heads = query_heads.reshape(seq_count, pair_len, group_width)
    own_keys = key_heads.reshape(seq_count, pair_len, group_width)
    own_values = value_heads.reshape(seq_count, pair_len, group_width)
    key_all, value_all = (
        lax.all_gather(
            own_keys.reshape(seq_count, 1, pair_len, group_width), "ctx", axis=1, tiled=True
        ),
        lax.all_gather(
            own_values.reshape(seq_count, 1, pair_len, group_width), "ctx", axis=1, tiled=True
        ),
    )
    key_all = key_all.reshape(seq_count, -1, group_width)
    value_all = value_all.reshape(seq_count, -1, group_width)
    attended, summary = lax.map(
        attend_forward, (query_heads, key_all, value_all, query_places, key_places)
    )
    attended_rows = lax.all_to_all(
        for_sending(to_pairs(attended)), "fsdp", split_axis=2, concat_axis=3, tiled=True
    ).reshape(-1, model_width)
    branch = jnp.dot(attended_rows, out_full, preferred_element_type=jnp.float32) + bias_out
    middle = inputs + branch
    normed_mlp, mlp_norm_back = jax.vjp(layer_norm, middle, gain_mlp, shift_mlp)
    mlp_low = normed_mlp.astype(jnp.bfloat16)
    hidden = jnp.dot(mlp_low, fc_full, preferred_element_type=jnp.float32) + bias_fc
    activated, gelu_back = jax.vjp(gelu_tanh, hidden)
    activated_low = activated.astype(jnp.bfloat16)
    result = (
        middle + jnp.dot(activated_low, proj_full, preferred_element_type=jnp.float32) + bias_proj
    )
    layer_out = result.astype(jnp.bfloat16).reshape(layer_in.shape)
    grad_rows = out_grad.reshape(-1, model_width)
    grad_result = grad_rows.astype(jnp.float32)
    proj_grad = contract_first(activated_low, grad_rows)
    proj_bias_grad = jnp.sum(grad_result, axis=0)
    grad_activated = contract_last(grad_rows, proj_full)
    grad_hidden = gelu_back(grad_activated)[0].astype(jnp.bfloat16)
    fc_grad = contract_first(mlp_low, grad_hidden)
    fc_bias_grad = jnp.sum(grad_hidden.astype(jnp.float32), axis=0)
    grad_middle, mlp_gain_grad, mlp_shift_grad = mlp_norm_back(contract_last(grad_hidden, fc_full))
    grad_middle = grad_middle + grad_result
    grad_branch = grad_middle.astype(jnp.bfloat16)
    out_weight_term = contract_first(attended_rows, grad_branch)
    out_bias_grad = jnp.sum(grad_branch.astype(jnp.float32), axis=0)
    grad_attended = contract_last(grad_branch, out_full).astype(jnp.bfloat16)
    grad_heads = lax.all_to_all(
        to_groups(grad_attended), "fsdp", split_axis=3, concat_axis=2, tiled=True
    ).reshape(seq_count, pair_len, group_width)
    grad_query, grad_keys, grad_values = lax.map(
        attend_backward,
        (query_heads, key_all, value_all, grad_heads, summary, query_places, key_places),
    )
    kv_grads = jnp.concatenate([grad_keys, grad_values], axis=2).astype(jnp.bfloat16)
    kv_grads = kv_grads.reshape(seq_count, ctx_size, pair_len, 2 * group_width).transpose(1, 0, 2, 3)
    kv_part = lax.psum_scatter(
        kv_grads.reshape(ctx_size * seq_count * pair_len, 2 * group_width),
        "ctx",
        scatter_dimension=0,
        tiled=True,
    ).reshape(seq_count, pair_len, 2 * group_width)
    key_part = kv_part[..., :group_width].astype(jnp.float32)
    value_part = kv_part[..., group_width:].astype(jnp.float32)
    key_grad_low = key_part.astype(jnp.bfloat16)
    value_grad_low = value_part.astype(jnp.bfloat16)
    query_back, key_back, value_back = (
        lax.all_to_all(
            for_sending(to_pairs(grad_query)), "fsdp", split_axis=2, concat_axis=3, tiled=True
        ),
        lax.all_to_all(
            for_sending(to_pairs(key_grad_low)), "fsdp", split_axis=2, concat_axis=3, tiled=True
        ),
        lax.all_to_all(
            for_sending(to_pairs(value_grad_low)), "fsdp", split_axis=2, concat_axis=3, tiled=True
        ),
    )
    grad_mixed = jnp.concatenate(
        [
            query_back.reshape(-1, model_width) * 0.125,
            key_back.reshape(-1, model_width),
            value_back.reshape(-1, model_width),
        ],
        axis=1,
    )
    qkv_grad = contract_first(normed_low, grad_mixed)
    mixed_float = grad_mixed.astype(jnp.float32)
    query_bias_grad = jnp.sum(mixed_float[:, :model_width], axis=0)
    value_bias_grad = jnp.sum(mixed_float[:, 2 * model_width :], axis=0)
    grad_inputs, attn_gain_grad, attn_shift_grad = attn_norm_back(
        contract_last(grad_mixed, qkv_full)
    )
    in_grad = (grad_inputs + grad_middle).reshape(layer_in.shape)
    shares = (
        lax.psum_scatter(
            qkv_grad.astype(jnp.bfloat16), "fsdp", scatter_dimension=0, tiled=True
        ).astype(jnp.float32),
        lax.psum_scatter(
            out_weight_term.astype(jnp.bfloat16), "fsdp", scatter_dimension=0, tiled=True
        ).astype(jnp.float32),
        lax.psum_scatter(
            fc_grad.astype(jnp.bfloat16), "fsdp", scatter_dimension=0, tiled=True
        ).astype(jnp.float32),
        lax.psum_scatter(
            proj_grad.astype(jnp.bfloat16), "fsdp", scatter_dimension=0, tiled=True
        ).astype(jnp.float32),
        lax.psum_scatter(
            attn_gain_grad.astype(jnp.bfloat16), "fsdp", scatter_dimension=0, tiled=True
        ).astype(jnp.float32),
        lax.psum_scatter(
            attn_shift_grad.astype(jnp.bfloat16), "fsdp", scatter_dimension=0, tiled=True
        ).astype(jnp.float32),
        lax.psum_scatter(
            query_bias_grad.astype(jnp.bfloat16), "fsdp", scatter_dimension=0, tiled=True
        ).astype(jnp.float32),
        lax.psum_scatter(
            value_bias_grad.astype(jnp.bfloat16), "fsdp", scatter_dimension=0, tiled=True
        ).astype(jnp.float32),
        lax.psum_scatter(
            out_bias_grad.astype(jnp.bfloat16), "fsdp", scatter_dimension=0, tiled=True
        ).astype(jnp.float32),
        lax.psum_scatter(
            mlp_gain_grad.astype(jnp.bfloat16), "fsdp", scatter_dimension=0, tiled=True
        ).astype(jnp.float32),
        lax.psum_scatter(
            mlp_shift_grad.astype(jnp.bfloat16), "fsdp", scatter_dimension=0, tiled=True
        ).astype(jnp.float32),
        lax.psum_scatter(
            fc_bias_grad.astype(jnp.bfloat16), "fsdp", scatter_dimension=0, tiled=True
        ).astype(jnp.float32),
        lax.psum_scatter(
            proj_bias_grad.astype(jnp.bfloat16), "fsdp", scatter_dimension=0, tiled=True
        ).astype(jnp.float32),
    )
    slices = (
        lax.psum_scatter(
            shares[0].astype(jnp.bfloat16), "ctx", scatter_dimension=0, tiled=True
        ).astype(jnp.float32),
        lax.psum_scatter(
            shares[1].astype(jnp.bfloat16), "ctx", scatter_dimension=0, tiled=True
        ).astype(jnp.float32),
        lax.psum_scatter(
            shares[2].astype(jnp.bfloat16), "ctx", scatter_dimension=0, tiled=True
        ).astype(jnp.float32),
        lax.psum_scatter(
            shares[3].astype(jnp.bfloat16), "ctx", scatter_dimension=0, tiled=True
        ).astype(jnp.float32),
        lax.psum_scatter(
            shares[4].astype(jnp.bfloat16), "ctx", scatter_dimension=0, tiled=True
        ).astype(jnp.float32),
        lax.psum_scatter(
            shares[5].astype(jnp.bfloat16), "ctx", scatter_dimension=0, tiled=True
        ).astype(jnp.float32),
        lax.psum_scatter(
            shares[6].astype(jnp.bfloat16), "ctx", scatter_dimension=0, tiled=True
        ).astype(jnp.float32),
        lax.psum_scatter(
            shares[7].astype(jnp.bfloat16), "ctx", scatter_dimension=0, tiled=True
        ).astype(jnp.float32),
        lax.psum_scatter(
            shares[8].astype(jnp.bfloat16), "ctx", scatter_dimension=0, tiled=True
        ).astype(jnp.float32),
        lax.psum_scatter(
            shares[9].astype(jnp.bfloat16), "ctx", scatter_dimension=0, tiled=True
        ).astype(jnp.float32),
        lax.psum_scatter(
            shares[10].astype(jnp.bfloat16), "ctx", scatter_dimension=0, tiled=True
        ).astype(jnp.float32),
        lax.psum_scatter(
            shares[11].astype(jnp.bfloat16), "ctx", scatter_dimension=0, tiled=True
        ).astype(jnp.float32),
        lax.psum_scatter(
            shares[12].astype(jnp.bfloat16), "ctx", scatter_dimension=0, tiled=True
        ).astype(jnp.float32),
    )
    totals = (
        lax.all_gather(slices[0].astype(jnp.bfloat16), "ctx", axis=0, tiled=True).astype(
            jnp.float32
        ),
        lax.all_gather(slices[1].astype(jnp.bfloat16), "ctx", axis=0, tiled=True).astype(
            jnp.float32
        ),
        lax.all_gather(slices[2].astype(jnp.bfloat16), "ctx", axis=0, tiled=True).astype(
            jnp.float32
        ),
        lax.all_gather(slices[3].astype(jnp.bfloat16), "ctx", axis=0, tiled=True).astype(
            jnp.float32
        ),
        lax.all_gather(slices[4].astype(jnp.bfloat16), "ctx", axis=0, tiled=True).astype(
            jnp.float32
        ),
        lax.all_gather(slices[5].astype(jnp.bfloat16), "ctx", axis=0, tiled=True).astype(
            jnp.float32
        ),
        lax.all_gather(slices[6].astype(jnp.bfloat16), "ctx", axis=0, tiled=True).astype(
            jnp.float32
        ),
        lax.all_gather(slices[7].astype(jnp.bfloat16), "ctx", axis=0, tiled=True).astype(
            jnp.float32
        ),
        lax.all_gather(slices[8].astype(jnp.bfloat16), "ctx", axis=0, tiled=True).astype(
            jnp.float32
        ),
        lax.all_gather(slices[9].astype(jnp.bfloat16), "ctx", axis=0, tiled=True).astype(
            jnp.float32
        ),
        lax.all_gather(slices[10].astype(jnp.bfloat16), "ctx", axis=0, tiled=True).astype(
            jnp.float32
        ),
        lax.all_gather(slices[11].astype(jnp.bfloat16), "ctx", axis=0, tiled=True).astype(
            jnp.float32
        ),
        lax.all_gather(slices[12].astype(jnp.bfloat16), "ctx", axis=0, tiled=True).astype(
            jnp.float32
        ),
    )
    return (
        layer_out,
        in_grad,
        totals[4],
        totals[5],
        totals[0],
        totals[6],
        totals[7],
        totals[1],
        totals[8],
        totals[9],
        totals[10],
        totals[2],
        totals[11],
        totals[3],
        totals[12],
    )


def solution(mesh):
    placed = (
        P(None, "ctx", None, "fsdp", None),
        P(None, "ctx", None, "fsdp", None),
        P(),
        P("fsdp"),
        P("fsdp"),
        P("fsdp", None),
        P("fsdp"),
        P("fsdp"),
        P("fsdp", None),
        P("fsdp"),
        P("fsdp"),
        P("fsdp"),
        P("fsdp", None),
        P("fsdp"),
        P("fsdp", None),
        P("fsdp"),
    )
    return jax.shard_map(
        shards,
        mesh=mesh,
        in_specs=placed,
        out_specs=(
            P(None, "ctx", None, "fsdp", None),
            P(None, "ctx", None, "fsdp", None),
            P("fsdp"),
            P("fsdp"),
            P("fsdp", None),
            P("fsdp"),
            P("fsdp"),
            P("fsdp", None),
            P("fsdp"),
            P("fsdp"),
            P("fsdp"),
            P("fsdp", None),
            P("fsdp"),
            P("fsdp", None),
            P("fsdp"),
        ),
        check_vma=False,
    )
```

```python
import jax
import jax.numpy as jnp
from jax import lax
from jax.sharding import PartitionSpec as P

HD = 64


norm_eps = 1e-05
masked_score = -1e30


def for_sending(array):
    return jax.tree.map(lambda a: a.astype(jnp.bfloat16) if a.dtype == jnp.float32 else a, array)


def layer_norm(values, gain, shift):
    average = jnp.mean(values, axis=-1, keepdims=True)
    centred = values - average
    spread = jnp.mean(centred * centred, axis=-1, keepdims=True)
    return centred * lax.rsqrt(spread + norm_eps) * gain + shift


def gelu_tanh(values):
    return jax.nn.gelu(values, approximate=True)


def contract_last(left, right):
    return lax.dot_general(
        left, right, (((1,), (1,)), ((), ())), preferred_element_type=jnp.float32
    )


def contract_first(left, right):
    return lax.dot_general(
        left, right, (((0,), (0,)), ((), ())), preferred_element_type=jnp.float32
    )


def head_scores(query, keys, query_places, key_places):
    scores = contract_last(query, keys)
    return jnp.where(key_places[None, :] <= query_places[:, None], scores, masked_score)


def score_grads(query, keys, values, grad_out, summary, row_sum, query_places, key_places):
    scores = head_scores(query, keys, query_places, key_places)
    probs = jnp.exp(scores - summary[:, None])
    grad_probs = contract_last(grad_out, values)
    row_sum = jnp.sum(probs * grad_probs, axis=1)
    grad_scores = (probs * (grad_probs - row_sum[:, None])).astype(jnp.bfloat16)
    return (probs.astype(jnp.bfloat16), grad_scores, row_sum)


def attend_forward(items):
    query, keys, values, query_places, key_places = items
    outputs = []
    summaries = []
    for head_index in range(query.shape[1] // HD):
        columns = slice(head_index * HD, (head_index + 1) * HD)
        scores = head_scores(query[:, columns], keys[:, columns], query_places, key_places)
        row_peak = jnp.max(scores, axis=1, keepdims=True)
        raised = jnp.exp(scores - row_peak)
        row_total = jnp.sum(raised, axis=1, keepdims=True)
        weights = (raised / row_total).astype(jnp.bfloat16)
        outputs.append(
            jnp.dot(weights, values[:, columns], preferred_element_type=jnp.float32).astype(
                jnp.bfloat16
            )
        )
        summaries.append(row_peak[:, 0] + jnp.log(row_total[:, 0]))
    return (jnp.concatenate(outputs, axis=1), jnp.stack(summaries, axis=1))


def attend_backward(items):
    query, keys, values, grad_out, summary, query_places, key_places = items
    query_parts, key_parts, value_parts = ([], [], [])
    for head_index in range(query.shape[1] // HD):
        columns = slice(head_index * HD, (head_index + 1) * HD)
        probs_low, grad_scores, row_sum = score_grads(
            query[:, columns],
            keys[:, columns],
            values[:, columns],
            grad_out[:, columns],
            summary[:, head_index],
            None,
            query_places,
            key_places,
        )
        query_parts.append(
            jnp.dot(grad_scores, keys[:, columns], preferred_element_type=jnp.float32).astype(
                jnp.bfloat16
            )
        )
        key_parts.append(contract_first(grad_scores, query[:, columns]))
        value_parts.append(contract_first(probs_low, grad_out[:, columns]))
    return (
        jnp.concatenate(query_parts, axis=1),
        jnp.concatenate(key_parts, axis=1),
        jnp.concatenate(value_parts, axis=1),
    )


CTX = ("zc", "core")


def gather_weight(shard):
    half = shard.shape[0] // 2
    piece = lax.dynamic_slice_in_dim(shard, lax.axis_index("core") * half, half, 0)
    pieces = lax.all_gather(piece, "fsdp", axis=0, tiled=False)
    whole = lax.all_gather(pieces, "core", axis=1, tiled=True)
    return whole.reshape(-1, shard.shape[1])


def core_major(rows, fsdp_size):
    count, width = rows.shape
    return rows.reshape(count, fsdp_size, 2, width // (2 * fsdp_size)).transpose(0, 2, 1, 3).reshape(
        count, width
    )


def reduce_weight_grad(grad):
    grad = lax.psum_scatter(grad.astype(jnp.bfloat16), "core", scatter_dimension=0, tiled=True)
    grad = lax.psum_scatter(grad, "fsdp", scatter_dimension=0, tiled=True)
    grad = lax.psum_scatter(grad, "zc", scatter_dimension=0, tiled=True)
    grad = lax.all_gather(grad, "zc", axis=0, tiled=True)
    grad = lax.all_gather(grad, "core", axis=0, tiled=True)
    return grad.astype(jnp.float32)


def shards(
    layer_in,
    out_grad,
    block_pairs,
    attn_gain,
    attn_shift,
    qkv_weight,
    query_bias,
    value_bias,
    out_weight,
    out_bias,
    mlp_gain,
    mlp_shift,
    fc_weight,
    fc_bias,
    proj_weight,
    proj_bias,
):
    fsdp_size = lax.axis_size("fsdp")
    ctx_size = lax.axis_size("zc") * lax.axis_size("core")
    seq_count = layer_in.shape[0]
    half_rows = layer_in.shape[3]
    model_width = layer_in.shape[4]
    block_len = half_rows * fsdp_size
    pair_len = 2 * block_len
    group_width = model_width // fsdp_size
    gathered = (
        gather_weight(qkv_weight),
        gather_weight(out_weight),
        gather_weight(fc_weight),
        gather_weight(proj_weight),
        lax.all_gather(attn_gain, "fsdp", axis=0, tiled=True),
        lax.all_gather(attn_shift, "fsdp", axis=0, tiled=True),
        lax.all_gather(query_bias, "fsdp", axis=0, tiled=True),
        lax.all_gather(value_bias, "fsdp", axis=0, tiled=True),
        lax.all_gather(out_bias, "fsdp", axis=0, tiled=True),
        lax.all_gather(mlp_gain, "fsdp", axis=0, tiled=True),
        lax.all_gather(mlp_shift, "fsdp", axis=0, tiled=True),
        lax.all_gather(fc_bias, "fsdp", axis=0, tiled=True),
        lax.all_gather(proj_bias, "fsdp", axis=0, tiled=True),
    )
    qkv_full, out_full, fc_full, proj_full = (gathered[0], gathered[1], gathered[2], gathered[3])
    vectors = [piece.astype(jnp.float32) for piece in gathered[4:]]
    (
        gain_attn,
        shift_attn,
        bias_query,
        bias_value,
        bias_out,
        gain_mlp,
        shift_mlp,
        bias_fc,
        bias_proj,
    ) = vectors
    halves = jnp.stack([block_pairs, 2 * ctx_size - 1 - block_pairs], axis=2)
    key_places = (halves[..., None] * block_len + jnp.arange(block_len, dtype=jnp.int32)).reshape(
        seq_count, ctx_size, pair_len
    )
    query_places = lax.dynamic_slice_in_dim(key_places, lax.axis_index(CTX), 1, 1).reshape(
        seq_count, pair_len
    )
    key_places = key_places.reshape(seq_count, ctx_size * pair_len)
    inputs = layer_in.reshape(-1, model_width).astype(jnp.float32)
    normed, attn_norm_back = jax.vjp(layer_norm, inputs, gain_attn, shift_attn)
    normed_low = normed.astype(jnp.bfloat16)
    mixed = jnp.dot(normed_low, qkv_full, preferred_element_type=jnp.float32)
    query = ((mixed[:, :model_width] + bias_query) * 0.125).astype(jnp.bfloat16)
    keys = mixed[:, model_width : 2 * model_width].astype(jnp.bfloat16)
    values = (mixed[:, 2 * model_width :] + bias_value).astype(jnp.bfloat16)

    def to_groups(array):
        return array.reshape(seq_count, 2, half_rows, fsdp_size, group_width)

    def to_pairs(array):
        return array.reshape(seq_count, 2, block_len, 1, group_width)

    query_heads, key_heads, value_heads = (
        lax.all_to_all(to_groups(query), "fsdp", split_axis=3, concat_axis=2, tiled=True),
        lax.all_to_all(to_groups(keys), "fsdp", split_axis=3, concat_axis=2, tiled=True),
        lax.all_to_all(to_groups(values), "fsdp", split_axis=3, concat_axis=2, tiled=True),
    )
    query_heads = query_heads.reshape(seq_count, pair_len, group_width)
    own_keys = key_heads.reshape(seq_count, pair_len, group_width)
    own_values = value_heads.reshape(seq_count, pair_len, group_width)
    key_all, value_all = (
        lax.all_gather(
            own_keys.reshape(seq_count, 1, pair_len, group_width), CTX, axis=1, tiled=True
        ),
        lax.all_gather(
            own_values.reshape(seq_count, 1, pair_len, group_width), CTX, axis=1, tiled=True
        ),
    )
    key_all = key_all.reshape(seq_count, -1, group_width)
    value_all = value_all.reshape(seq_count, -1, group_width)
    attended, summary = lax.map(
        attend_forward, (query_heads, key_all, value_all, query_places, key_places)
    )
    attended_rows = lax.all_to_all(
        for_sending(to_pairs(attended)), "fsdp", split_axis=2, concat_axis=3, tiled=True
    ).reshape(-1, model_width)
    branch = jnp.dot(attended_rows, out_full, preferred_element_type=jnp.float32) + bias_out
    middle = inputs + branch
    normed_mlp, mlp_norm_back = jax.vjp(layer_norm, middle, gain_mlp, shift_mlp)
    mlp_low = normed_mlp.astype(jnp.bfloat16)
    hidden = jnp.dot(mlp_low, fc_full, preferred_element_type=jnp.float32) + bias_fc
    activated, gelu_back = jax.vjp(gelu_tanh, hidden)
    activated_low = activated.astype(jnp.bfloat16)
    result = (
        middle + jnp.dot(activated_low, proj_full, preferred_element_type=jnp.float32) + bias_proj
    )
    layer_out = result.astype(jnp.bfloat16).reshape(layer_in.shape)
    grad_rows = out_grad.reshape(-1, model_width)
    grad_result = grad_rows.astype(jnp.float32)
    proj_grad = contract_first(core_major(activated_low, fsdp_size), grad_rows)
    proj_bias_grad = jnp.sum(grad_result, axis=0)
    grad_activated = contract_last(grad_rows, proj_full)
    grad_hidden = gelu_back(grad_activated)[0].astype(jnp.bfloat16)
    fc_grad = contract_first(core_major(mlp_low, fsdp_size), grad_hidden)
    fc_bias_grad = jnp.sum(grad_hidden.astype(jnp.float32), axis=0)
    grad_middle, mlp_gain_grad, mlp_shift_grad = mlp_norm_back(contract_last(grad_hidden, fc_full))
    grad_middle = grad_middle + grad_result
    grad_branch = grad_middle.astype(jnp.bfloat16)
    out_weight_term = contract_first(core_major(attended_rows, fsdp_size), grad_branch)
    out_bias_grad = jnp.sum(grad_branch.astype(jnp.float32), axis=0)
    grad_attended = contract_last(grad_branch, out_full).astype(jnp.bfloat16)
    grad_heads = lax.all_to_all(
        to_groups(grad_attended), "fsdp", split_axis=3, concat_axis=2, tiled=True
    ).reshape(seq_count, pair_len, group_width)
    grad_query, grad_keys, grad_values = lax.map(
        attend_backward,
        (query_heads, key_all, value_all, grad_heads, summary, query_places, key_places),
    )
    kv_grads = jnp.concatenate([grad_keys, grad_values], axis=2).astype(jnp.bfloat16)
    kv_grads = kv_grads.reshape(seq_count, ctx_size, pair_len, 2 * group_width).transpose(1, 0, 2, 3)
    kv_part = lax.psum_scatter(
        kv_grads.reshape(ctx_size * seq_count * pair_len, 2 * group_width),
        CTX,
        scatter_dimension=0,
        tiled=True,
    ).reshape(seq_count, pair_len, 2 * group_width)
    key_part = kv_part[..., :group_width].astype(jnp.float32)
    value_part = kv_part[..., group_width:].astype(jnp.float32)
    key_grad_low = key_part.astype(jnp.bfloat16)
    value_grad_low = value_part.astype(jnp.bfloat16)
    query_back, key_back, value_back = (
        lax.all_to_all(
            for_sending(to_pairs(grad_query)), "fsdp", split_axis=2, concat_axis=3, tiled=True
        ),
        lax.all_to_all(
            for_sending(to_pairs(key_grad_low)), "fsdp", split_axis=2, concat_axis=3, tiled=True
        ),
        lax.all_to_all(
            for_sending(to_pairs(value_grad_low)), "fsdp", split_axis=2, concat_axis=3, tiled=True
        ),
    )
    grad_mixed = jnp.concatenate(
        [
            query_back.reshape(-1, model_width) * 0.125,
            key_back.reshape(-1, model_width),
            value_back.reshape(-1, model_width),
        ],
        axis=1,
    )
    qkv_grad = contract_first(core_major(normed_low, fsdp_size), grad_mixed)
    mixed_float = grad_mixed.astype(jnp.float32)
    query_bias_grad = jnp.sum(mixed_float[:, :model_width], axis=0)
    value_bias_grad = jnp.sum(mixed_float[:, 2 * model_width :], axis=0)
    grad_inputs, attn_gain_grad, attn_shift_grad = attn_norm_back(
        contract_last(grad_mixed, qkv_full)
    )
    in_grad = (grad_inputs + grad_middle).reshape(layer_in.shape)
    weight_totals = tuple(
        reduce_weight_grad(grad) for grad in (qkv_grad, out_weight_term, fc_grad, proj_grad)
    )
    vector_totals = []
    for grad in (
        attn_gain_grad,
        attn_shift_grad,
        query_bias_grad,
        value_bias_grad,
        out_bias_grad,
        mlp_gain_grad,
        mlp_shift_grad,
        fc_bias_grad,
        proj_bias_grad,
    ):
        share = lax.psum_scatter(grad.astype(jnp.bfloat16), "fsdp", scatter_dimension=0, tiled=True)
        piece = lax.psum_scatter(share, CTX, scatter_dimension=0, tiled=True)
        vector_totals.append(lax.all_gather(piece, CTX, axis=0, tiled=True).astype(jnp.float32))
    totals = weight_totals + tuple(vector_totals)
    return (
        layer_out,
        in_grad,
        totals[4],
        totals[5],
        totals[0],
        totals[6],
        totals[7],
        totals[1],
        totals[8],
        totals[9],
        totals[10],
        totals[2],
        totals[11],
        totals[3],
        totals[12],
    )


def solution(mesh):
    ctx_count, fsdp_count = mesh.devices.shape
    mesh = jax.sharding.Mesh(
        mesh.devices.reshape(ctx_count // 2, 2, fsdp_count), ("zc", "core", "fsdp")
    )
    placed = (
        P(None, CTX, None, "fsdp", None),
        P(None, CTX, None, "fsdp", None),
        P(),
        P("fsdp"),
        P("fsdp"),
        P("fsdp", None),
        P("fsdp"),
        P("fsdp"),
        P("fsdp", None),
        P("fsdp"),
        P("fsdp"),
        P("fsdp"),
        P("fsdp", None),
        P("fsdp"),
        P("fsdp", None),
        P("fsdp"),
    )
    return jax.shard_map(
        shards,
        mesh=mesh,
        in_specs=placed,
        out_specs=(
            P(None, CTX, None, "fsdp", None),
            P(None, CTX, None, "fsdp", None),
            P("fsdp"),
            P("fsdp"),
            P("fsdp", None),
            P("fsdp"),
            P("fsdp"),
            P("fsdp", None),
            P("fsdp"),
            P("fsdp"),
            P("fsdp"),
            P("fsdp", None),
            P("fsdp"),
            P("fsdp", None),
            P("fsdp"),
        ),
        check_vma=False,
    )
```

```python
import jax
import jax.numpy as jnp
from jax import lax
from jax.sharding import PartitionSpec as P

HD = 64


norm_eps = 1e-05
masked_score = -1e30


def for_sending(array):
    return jax.tree.map(lambda a: a.astype(jnp.bfloat16) if a.dtype == jnp.float32 else a, array)


def layer_norm(values, gain, shift):
    average = jnp.mean(values, axis=-1, keepdims=True)
    centred = values - average
    spread = jnp.mean(centred * centred, axis=-1, keepdims=True)
    return centred * lax.rsqrt(spread + norm_eps) * gain + shift


def gelu_tanh(values):
    return jax.nn.gelu(values, approximate=True)


def contract_last(left, right):
    return lax.dot_general(
        left, right, (((1,), (1,)), ((), ())), preferred_element_type=jnp.float32
    )


def contract_first(left, right):
    return lax.dot_general(
        left, right, (((0,), (0,)), ((), ())), preferred_element_type=jnp.float32
    )


def head_scores(query, keys, query_places, key_places):
    scores = contract_last(query, keys)
    return jnp.where(key_places[None, :] <= query_places[:, None], scores, masked_score)


def score_grads(query, keys, values, grad_out, summary, row_sum, query_places, key_places):
    scores = head_scores(query, keys, query_places, key_places)
    probs = jnp.exp(scores - summary[:, None])
    grad_probs = contract_last(grad_out, values)
    row_sum = jnp.sum(probs * grad_probs, axis=1)
    grad_scores = (probs * (grad_probs - row_sum[:, None])).astype(jnp.bfloat16)
    return (probs.astype(jnp.bfloat16), grad_scores, row_sum)


def attend_forward(items):
    query, keys, values, query_places, key_places = items
    outputs = []
    summaries = []
    for head_index in range(query.shape[1] // HD):
        columns = slice(head_index * HD, (head_index + 1) * HD)
        scores = head_scores(query[:, columns], keys[:, columns], query_places, key_places)
        row_peak = jnp.max(scores, axis=1, keepdims=True)
        raised = jnp.exp(scores - row_peak)
        row_total = jnp.sum(raised, axis=1, keepdims=True)
        weights = (raised / row_total).astype(jnp.bfloat16)
        outputs.append(
            jnp.dot(weights, values[:, columns], preferred_element_type=jnp.float32).astype(
                jnp.bfloat16
            )
        )
        summaries.append(row_peak[:, 0] + jnp.log(row_total[:, 0]))
    return (jnp.concatenate(outputs, axis=1), jnp.stack(summaries, axis=1))


def attend_backward(items):
    query, keys, values, grad_out, summary, query_places, key_places = items
    query_parts, key_parts, value_parts = ([], [], [])
    for head_index in range(query.shape[1] // HD):
        columns = slice(head_index * HD, (head_index + 1) * HD)
        probs_low, grad_scores, row_sum = score_grads(
            query[:, columns],
            keys[:, columns],
            values[:, columns],
            grad_out[:, columns],
            summary[:, head_index],
            None,
            query_places,
            key_places,
        )
        query_parts.append(
            jnp.dot(grad_scores, keys[:, columns], preferred_element_type=jnp.float32).astype(
                jnp.bfloat16
            )
        )
        key_parts.append(contract_first(grad_scores, query[:, columns]))
        value_parts.append(contract_first(probs_low, grad_out[:, columns]))
    return (
        jnp.concatenate(query_parts, axis=1),
        jnp.concatenate(key_parts, axis=1),
        jnp.concatenate(value_parts, axis=1),
    )


CTX = ("zc", "core")


def gather_weight(shard):
    half = shard.shape[0] // 2
    piece = lax.dynamic_slice_in_dim(shard, lax.axis_index("core") * half, half, 0)
    fsdp_size = lax.axis_size("fsdp")
    pieces = lax.all_to_all(
        jnp.broadcast_to(piece[None], (fsdp_size,) + piece.shape),
        "fsdp",
        split_axis=0,
        concat_axis=0,
        tiled=True,
    )
    whole = lax.all_gather(pieces, "core", axis=1, tiled=True)
    return whole.reshape(-1, shard.shape[1])


def core_major(rows, fsdp_size):
    count, width = rows.shape
    return rows.reshape(count, fsdp_size, 2, width // (2 * fsdp_size)).transpose(0, 2, 1, 3).reshape(
        count, width
    )


def reduce_weight_grad(grad):
    grad = lax.psum_scatter(grad.astype(jnp.bfloat16), "core", scatter_dimension=0, tiled=True)
    grad = lax.psum_scatter(grad, "fsdp", scatter_dimension=0, tiled=True)
    grad = lax.psum_scatter(grad, "zc", scatter_dimension=0, tiled=True)
    grad = lax.all_gather(grad, "zc", axis=0, tiled=True)
    grad = lax.all_gather(grad, "core", axis=0, tiled=True)
    return grad.astype(jnp.float32)


def shards(
    layer_in,
    out_grad,
    block_pairs,
    attn_gain,
    attn_shift,
    qkv_weight,
    query_bias,
    value_bias,
    out_weight,
    out_bias,
    mlp_gain,
    mlp_shift,
    fc_weight,
    fc_bias,
    proj_weight,
    proj_bias,
):
    fsdp_size = lax.axis_size("fsdp")
    ctx_size = lax.axis_size("zc") * lax.axis_size("core")
    seq_count = layer_in.shape[0]
    half_rows = layer_in.shape[3]
    model_width = layer_in.shape[4]
    block_len = half_rows * fsdp_size
    pair_len = 2 * block_len
    group_width = model_width // fsdp_size
    gathered = (
        gather_weight(qkv_weight),
        gather_weight(out_weight),
        gather_weight(fc_weight),
        gather_weight(proj_weight),
        lax.all_gather(attn_gain, "fsdp", axis=0, tiled=True),
        lax.all_gather(attn_shift, "fsdp", axis=0, tiled=True),
        lax.all_gather(query_bias, "fsdp", axis=0, tiled=True),
        lax.all_gather(value_bias, "fsdp", axis=0, tiled=True),
        lax.all_gather(out_bias, "fsdp", axis=0, tiled=True),
        lax.all_gather(mlp_gain, "fsdp", axis=0, tiled=True),
        lax.all_gather(mlp_shift, "fsdp", axis=0, tiled=True),
        lax.all_gather(fc_bias, "fsdp", axis=0, tiled=True),
        lax.all_gather(proj_bias, "fsdp", axis=0, tiled=True),
    )
    qkv_full, out_full, fc_full, proj_full = (gathered[0], gathered[1], gathered[2], gathered[3])
    vectors = [piece.astype(jnp.float32) for piece in gathered[4:]]
    (
        gain_attn,
        shift_attn,
        bias_query,
        bias_value,
        bias_out,
        gain_mlp,
        shift_mlp,
        bias_fc,
        bias_proj,
    ) = vectors
    halves = jnp.stack([block_pairs, 2 * ctx_size - 1 - block_pairs], axis=2)
    key_places = (halves[..., None] * block_len + jnp.arange(block_len, dtype=jnp.int32)).reshape(
        seq_count, ctx_size, pair_len
    )
    query_places = lax.dynamic_slice_in_dim(key_places, lax.axis_index(CTX), 1, 1).reshape(
        seq_count, pair_len
    )
    key_places = key_places.reshape(seq_count, ctx_size * pair_len)
    inputs = layer_in.reshape(-1, model_width).astype(jnp.float32)
    normed, attn_norm_back = jax.vjp(layer_norm, inputs, gain_attn, shift_attn)
    normed_low = normed.astype(jnp.bfloat16)
    mixed = jnp.dot(normed_low, qkv_full, preferred_element_type=jnp.float32)
    query = ((mixed[:, :model_width] + bias_query) * 0.125).astype(jnp.bfloat16)
    keys = mixed[:, model_width : 2 * model_width].astype(jnp.bfloat16)
    values = (mixed[:, 2 * model_width :] + bias_value).astype(jnp.bfloat16)

    def to_groups(array):
        return array.reshape(seq_count, 2, half_rows, fsdp_size, group_width)

    def to_pairs(array):
        return array.reshape(seq_count, 2, block_len, 1, group_width)

    query_heads, key_heads, value_heads = (
        lax.all_to_all(to_groups(query), "fsdp", split_axis=3, concat_axis=2, tiled=True),
        lax.all_to_all(to_groups(keys), "fsdp", split_axis=3, concat_axis=2, tiled=True),
        lax.all_to_all(to_groups(values), "fsdp", split_axis=3, concat_axis=2, tiled=True),
    )
    query_heads = query_heads.reshape(seq_count, pair_len, group_width)
    own_keys = key_heads.reshape(seq_count, pair_len, group_width)
    own_values = value_heads.reshape(seq_count, pair_len, group_width)
    key_all, value_all = (
        lax.all_gather(
            own_keys.reshape(seq_count, 1, pair_len, group_width), CTX, axis=1, tiled=True
        ),
        lax.all_gather(
            own_values.reshape(seq_count, 1, pair_len, group_width), CTX, axis=1, tiled=True
        ),
    )
    key_all = key_all.reshape(seq_count, -1, group_width)
    value_all = value_all.reshape(seq_count, -1, group_width)
    attended, summary = lax.map(
        attend_forward, (query_heads, key_all, value_all, query_places, key_places)
    )
    attended_rows = lax.all_to_all(
        for_sending(to_pairs(attended)), "fsdp", split_axis=2, concat_axis=3, tiled=True
    ).reshape(-1, model_width)
    branch = jnp.dot(attended_rows, out_full, preferred_element_type=jnp.float32) + bias_out
    middle = inputs + branch
    normed_mlp, mlp_norm_back = jax.vjp(layer_norm, middle, gain_mlp, shift_mlp)
    mlp_low = normed_mlp.astype(jnp.bfloat16)
    hidden = jnp.dot(mlp_low, fc_full, preferred_element_type=jnp.float32) + bias_fc
    activated, gelu_back = jax.vjp(gelu_tanh, hidden)
    activated_low = activated.astype(jnp.bfloat16)
    result = (
        middle + jnp.dot(activated_low, proj_full, preferred_element_type=jnp.float32) + bias_proj
    )
    layer_out = result.astype(jnp.bfloat16).reshape(layer_in.shape)
    grad_rows = out_grad.reshape(-1, model_width)
    grad_result = grad_rows.astype(jnp.float32)
    proj_grad = contract_first(core_major(activated_low, fsdp_size), grad_rows)
    proj_bias_grad = jnp.sum(grad_result, axis=0)
    grad_activated = contract_last(grad_rows, proj_full)
    grad_hidden = gelu_back(grad_activated)[0].astype(jnp.bfloat16)
    fc_grad = contract_first(core_major(mlp_low, fsdp_size), grad_hidden)
    fc_bias_grad = jnp.sum(grad_hidden.astype(jnp.float32), axis=0)
    grad_middle, mlp_gain_grad, mlp_shift_grad = mlp_norm_back(contract_last(grad_hidden, fc_full))
    grad_middle = grad_middle + grad_result
    grad_branch = grad_middle.astype(jnp.bfloat16)
    out_weight_term = contract_first(core_major(attended_rows, fsdp_size), grad_branch)
    out_bias_grad = jnp.sum(grad_branch.astype(jnp.float32), axis=0)
    grad_attended = contract_last(grad_branch, out_full).astype(jnp.bfloat16)
    grad_heads = lax.all_to_all(
        to_groups(grad_attended), "fsdp", split_axis=3, concat_axis=2, tiled=True
    ).reshape(seq_count, pair_len, group_width)
    grad_query, grad_keys, grad_values = lax.map(
        attend_backward,
        (query_heads, key_all, value_all, grad_heads, summary, query_places, key_places),
    )
    kv_grads = jnp.concatenate([grad_keys, grad_values], axis=2).astype(jnp.bfloat16)
    kv_grads = kv_grads.reshape(seq_count, ctx_size, pair_len, 2 * group_width).transpose(1, 0, 2, 3)
    kv_part = lax.psum_scatter(
        kv_grads.reshape(ctx_size * seq_count * pair_len, 2 * group_width),
        CTX,
        scatter_dimension=0,
        tiled=True,
    ).reshape(seq_count, pair_len, 2 * group_width)
    key_part = kv_part[..., :group_width].astype(jnp.float32)
    value_part = kv_part[..., group_width:].astype(jnp.float32)
    key_grad_low = key_part.astype(jnp.bfloat16)
    value_grad_low = value_part.astype(jnp.bfloat16)
    query_back, key_back, value_back = (
        lax.all_to_all(
            for_sending(to_pairs(grad_query)), "fsdp", split_axis=2, concat_axis=3, tiled=True
        ),
        lax.all_to_all(
            for_sending(to_pairs(key_grad_low)), "fsdp", split_axis=2, concat_axis=3, tiled=True
        ),
        lax.all_to_all(
            for_sending(to_pairs(value_grad_low)), "fsdp", split_axis=2, concat_axis=3, tiled=True
        ),
    )
    grad_mixed = jnp.concatenate(
        [
            query_back.reshape(-1, model_width) * 0.125,
            key_back.reshape(-1, model_width),
            value_back.reshape(-1, model_width),
        ],
        axis=1,
    )
    qkv_grad = contract_first(core_major(normed_low, fsdp_size), grad_mixed)
    mixed_float = grad_mixed.astype(jnp.float32)
    query_bias_grad = jnp.sum(mixed_float[:, :model_width], axis=0)
    value_bias_grad = jnp.sum(mixed_float[:, 2 * model_width :], axis=0)
    grad_inputs, attn_gain_grad, attn_shift_grad = attn_norm_back(
        contract_last(grad_mixed, qkv_full)
    )
    in_grad = (grad_inputs + grad_middle).reshape(layer_in.shape)
    weight_totals = tuple(
        reduce_weight_grad(grad) for grad in (qkv_grad, out_weight_term, fc_grad, proj_grad)
    )
    vector_totals = []
    for grad in (
        attn_gain_grad,
        attn_shift_grad,
        query_bias_grad,
        value_bias_grad,
        out_bias_grad,
        mlp_gain_grad,
        mlp_shift_grad,
        fc_bias_grad,
        proj_bias_grad,
    ):
        share = lax.psum_scatter(grad.astype(jnp.bfloat16), "fsdp", scatter_dimension=0, tiled=True)
        piece = lax.psum_scatter(share, CTX, scatter_dimension=0, tiled=True)
        vector_totals.append(lax.all_gather(piece, CTX, axis=0, tiled=True).astype(jnp.float32))
    totals = weight_totals + tuple(vector_totals)
    return (
        layer_out,
        in_grad,
        totals[4],
        totals[5],
        totals[0],
        totals[6],
        totals[7],
        totals[1],
        totals[8],
        totals[9],
        totals[10],
        totals[2],
        totals[11],
        totals[3],
        totals[12],
    )


def solution(mesh):
    ctx_count, fsdp_count = mesh.devices.shape
    mesh = jax.sharding.Mesh(
        mesh.devices.reshape(ctx_count // 2, 2, fsdp_count), ("zc", "core", "fsdp")
    )
    placed = (
        P(None, CTX, None, "fsdp", None),
        P(None, CTX, None, "fsdp", None),
        P(),
        P("fsdp"),
        P("fsdp"),
        P("fsdp", None),
        P("fsdp"),
        P("fsdp"),
        P("fsdp", None),
        P("fsdp"),
        P("fsdp"),
        P("fsdp"),
        P("fsdp", None),
        P("fsdp"),
        P("fsdp", None),
        P("fsdp"),
    )
    return jax.shard_map(
        shards,
        mesh=mesh,
        in_specs=placed,
        out_specs=(
            P(None, CTX, None, "fsdp", None),
            P(None, CTX, None, "fsdp", None),
            P("fsdp"),
            P("fsdp"),
            P("fsdp", None),
            P("fsdp"),
            P("fsdp"),
            P("fsdp", None),
            P("fsdp"),
            P("fsdp"),
            P("fsdp"),
            P("fsdp", None),
            P("fsdp"),
            P("fsdp", None),
            P("fsdp"),
        ),
        check_vma=False,
    )
```

```python
import jax
import jax.numpy as jnp
from jax import lax
from jax.sharding import PartitionSpec as P

HD = 64


norm_eps = 1e-05
masked_score = -1e30


def for_sending(array):
    return jax.tree.map(lambda a: a.astype(jnp.bfloat16) if a.dtype == jnp.float32 else a, array)


def layer_norm(values, gain, shift):
    average = jnp.mean(values, axis=-1, keepdims=True)
    centred = values - average
    spread = jnp.mean(centred * centred, axis=-1, keepdims=True)
    return centred * lax.rsqrt(spread + norm_eps) * gain + shift


def gelu_tanh(values):
    return jax.nn.gelu(values, approximate=True)


def contract_last(left, right):
    return lax.dot_general(
        left, right, (((1,), (1,)), ((), ())), preferred_element_type=jnp.float32
    )


def contract_first(left, right):
    return lax.dot_general(
        left, right, (((0,), (0,)), ((), ())), preferred_element_type=jnp.float32
    )


def head_scores(query, keys, query_places, key_places):
    scores = contract_last(query, keys)
    return jnp.where(key_places[None, :] <= query_places[:, None], scores, masked_score)


def score_grads(query, keys, values, grad_out, summary, row_sum, query_places, key_places):
    scores = head_scores(query, keys, query_places, key_places)
    probs = jnp.exp(scores - summary[:, None])
    grad_probs = contract_last(grad_out, values)
    row_sum = jnp.sum(probs * grad_probs, axis=1)
    grad_scores = (probs * (grad_probs - row_sum[:, None])).astype(jnp.bfloat16)
    return (probs.astype(jnp.bfloat16), grad_scores, row_sum)


def attend_forward(items):
    query, keys, values, query_places, key_places = items
    outputs = []
    summaries = []
    for head_index in range(query.shape[1] // HD):
        columns = slice(head_index * HD, (head_index + 1) * HD)
        scores = head_scores(query[:, columns], keys[:, columns], query_places, key_places)
        row_peak = jnp.max(scores, axis=1, keepdims=True)
        raised = jnp.exp(scores - row_peak)
        row_total = jnp.sum(raised, axis=1, keepdims=True)
        weights = (raised / row_total).astype(jnp.bfloat16)
        outputs.append(
            jnp.dot(weights, values[:, columns], preferred_element_type=jnp.float32).astype(
                jnp.bfloat16
            )
        )
        summaries.append(row_peak[:, 0] + jnp.log(row_total[:, 0]))
    return (jnp.concatenate(outputs, axis=1), jnp.stack(summaries, axis=1))


def attend_backward(items):
    query, keys, values, grad_out, summary, query_places, key_places = items
    query_parts, key_parts, value_parts = ([], [], [])
    for head_index in range(query.shape[1] // HD):
        columns = slice(head_index * HD, (head_index + 1) * HD)
        probs_low, grad_scores, row_sum = score_grads(
            query[:, columns],
            keys[:, columns],
            values[:, columns],
            grad_out[:, columns],
            summary[:, head_index],
            None,
            query_places,
            key_places,
        )
        query_parts.append(
            jnp.dot(grad_scores, keys[:, columns], preferred_element_type=jnp.float32).astype(
                jnp.bfloat16
            )
        )
        key_parts.append(contract_first(grad_scores, query[:, columns]))
        value_parts.append(contract_first(probs_low, grad_out[:, columns]))
    return (
        jnp.concatenate(query_parts, axis=1),
        jnp.concatenate(key_parts, axis=1),
        jnp.concatenate(value_parts, axis=1),
    )


CTX = ("zc", "core")


def gather_weight(shard):
    half = shard.shape[0] // 2
    piece = lax.dynamic_slice_in_dim(shard, lax.axis_index("core") * half, half, 0)
    fsdp_size = lax.axis_size("fsdp")
    pieces = lax.all_to_all(
        jnp.broadcast_to(piece[None], (fsdp_size,) + piece.shape),
        "fsdp",
        split_axis=0,
        concat_axis=0,
        tiled=True,
    )
    whole = lax.all_gather(pieces, "core", axis=1, tiled=True)
    return whole.reshape(-1, shard.shape[1])


def core_major(rows, fsdp_size):
    count, width = rows.shape
    return rows.reshape(count, fsdp_size, 2, width // (2 * fsdp_size)).transpose(0, 2, 1, 3).reshape(
        count, width
    )


def reduce_weight_grad(grad):
    grad = lax.psum_scatter(grad.astype(jnp.bfloat16), "core", scatter_dimension=0, tiled=True)
    fsdp_size = lax.axis_size("fsdp")
    blocks = lax.all_to_all(
        grad.reshape((fsdp_size, -1) + grad.shape[1:]), "fsdp", split_axis=0, concat_axis=0, tiled=True
    )
    grad = jnp.sum(blocks.astype(jnp.float32), axis=0).astype(jnp.bfloat16)
    grad = lax.psum_scatter(grad, "zc", scatter_dimension=0, tiled=True)
    grad = lax.all_gather(grad, "zc", axis=0, tiled=True)
    grad = lax.all_gather(grad, "core", axis=0, tiled=True)
    return grad.astype(jnp.float32)


def shards(
    layer_in,
    out_grad,
    block_pairs,
    attn_gain,
    attn_shift,
    qkv_weight,
    query_bias,
    value_bias,
    out_weight,
    out_bias,
    mlp_gain,
    mlp_shift,
    fc_weight,
    fc_bias,
    proj_weight,
    proj_bias,
):
    fsdp_size = lax.axis_size("fsdp")
    ctx_size = lax.axis_size("zc") * lax.axis_size("core")
    seq_count = layer_in.shape[0]
    half_rows = layer_in.shape[3]
    model_width = layer_in.shape[4]
    block_len = half_rows * fsdp_size
    pair_len = 2 * block_len
    group_width = model_width // fsdp_size
    gathered = (
        gather_weight(qkv_weight),
        gather_weight(out_weight),
        gather_weight(fc_weight),
        gather_weight(proj_weight),
        lax.all_gather(attn_gain, "fsdp", axis=0, tiled=True),
        lax.all_gather(attn_shift, "fsdp", axis=0, tiled=True),
        lax.all_gather(query_bias, "fsdp", axis=0, tiled=True),
        lax.all_gather(value_bias, "fsdp", axis=0, tiled=True),
        lax.all_gather(out_bias, "fsdp", axis=0, tiled=True),
        lax.all_gather(mlp_gain, "fsdp", axis=0, tiled=True),
        lax.all_gather(mlp_shift, "fsdp", axis=0, tiled=True),
        lax.all_gather(fc_bias, "fsdp", axis=0, tiled=True),
        lax.all_gather(proj_bias, "fsdp", axis=0, tiled=True),
    )
    qkv_full, out_full, fc_full, proj_full = (gathered[0], gathered[1], gathered[2], gathered[3])
    vectors = [piece.astype(jnp.float32) for piece in gathered[4:]]
    (
        gain_attn,
        shift_attn,
        bias_query,
        bias_value,
        bias_out,
        gain_mlp,
        shift_mlp,
        bias_fc,
        bias_proj,
    ) = vectors
    halves = jnp.stack([block_pairs, 2 * ctx_size - 1 - block_pairs], axis=2)
    key_places = (halves[..., None] * block_len + jnp.arange(block_len, dtype=jnp.int32)).reshape(
        seq_count, ctx_size, pair_len
    )
    query_places = lax.dynamic_slice_in_dim(key_places, lax.axis_index(CTX), 1, 1).reshape(
        seq_count, pair_len
    )
    key_places = key_places.reshape(seq_count, ctx_size * pair_len)
    inputs = layer_in.reshape(-1, model_width).astype(jnp.float32)
    normed, attn_norm_back = jax.vjp(layer_norm, inputs, gain_attn, shift_attn)
    normed_low = normed.astype(jnp.bfloat16)
    mixed = jnp.dot(normed_low, qkv_full, preferred_element_type=jnp.float32)
    query = ((mixed[:, :model_width] + bias_query) * 0.125).astype(jnp.bfloat16)
    keys = mixed[:, model_width : 2 * model_width].astype(jnp.bfloat16)
    values = (mixed[:, 2 * model_width :] + bias_value).astype(jnp.bfloat16)

    def to_groups(array):
        return array.reshape(seq_count, 2, half_rows, fsdp_size, group_width)

    def to_pairs(array):
        return array.reshape(seq_count, 2, block_len, 1, group_width)

    query_heads, key_heads, value_heads = (
        lax.all_to_all(to_groups(query), "fsdp", split_axis=3, concat_axis=2, tiled=True),
        lax.all_to_all(to_groups(keys), "fsdp", split_axis=3, concat_axis=2, tiled=True),
        lax.all_to_all(to_groups(values), "fsdp", split_axis=3, concat_axis=2, tiled=True),
    )
    query_heads = query_heads.reshape(seq_count, pair_len, group_width)
    own_keys = key_heads.reshape(seq_count, pair_len, group_width)
    own_values = value_heads.reshape(seq_count, pair_len, group_width)
    key_all, value_all = (
        lax.all_gather(
            own_keys.reshape(seq_count, 1, pair_len, group_width), CTX, axis=1, tiled=True
        ),
        lax.all_gather(
            own_values.reshape(seq_count, 1, pair_len, group_width), CTX, axis=1, tiled=True
        ),
    )
    key_all = key_all.reshape(seq_count, -1, group_width)
    value_all = value_all.reshape(seq_count, -1, group_width)
    attended, summary = lax.map(
        attend_forward, (query_heads, key_all, value_all, query_places, key_places)
    )
    attended_rows = lax.all_to_all(
        for_sending(to_pairs(attended)), "fsdp", split_axis=2, concat_axis=3, tiled=True
    ).reshape(-1, model_width)
    branch = jnp.dot(attended_rows, out_full, preferred_element_type=jnp.float32) + bias_out
    middle = inputs + branch
    normed_mlp, mlp_norm_back = jax.vjp(layer_norm, middle, gain_mlp, shift_mlp)
    mlp_low = normed_mlp.astype(jnp.bfloat16)
    hidden = jnp.dot(mlp_low, fc_full, preferred_element_type=jnp.float32) + bias_fc
    activated, gelu_back = jax.vjp(gelu_tanh, hidden)
    activated_low = activated.astype(jnp.bfloat16)
    result = (
        middle + jnp.dot(activated_low, proj_full, preferred_element_type=jnp.float32) + bias_proj
    )
    layer_out = result.astype(jnp.bfloat16).reshape(layer_in.shape)
    grad_rows = out_grad.reshape(-1, model_width)
    grad_result = grad_rows.astype(jnp.float32)
    proj_grad = contract_first(core_major(activated_low, fsdp_size), grad_rows)
    proj_bias_grad = jnp.sum(grad_result, axis=0)
    grad_activated = contract_last(grad_rows, proj_full)
    grad_hidden = gelu_back(grad_activated)[0].astype(jnp.bfloat16)
    fc_grad = contract_first(core_major(mlp_low, fsdp_size), grad_hidden)
    fc_bias_grad = jnp.sum(grad_hidden.astype(jnp.float32), axis=0)
    grad_middle, mlp_gain_grad, mlp_shift_grad = mlp_norm_back(contract_last(grad_hidden, fc_full))
    grad_middle = grad_middle + grad_result
    grad_branch = grad_middle.astype(jnp.bfloat16)
    out_weight_term = contract_first(core_major(attended_rows, fsdp_size), grad_branch)
    out_bias_grad = jnp.sum(grad_branch.astype(jnp.float32), axis=0)
    grad_attended = contract_last(grad_branch, out_full).astype(jnp.bfloat16)
    grad_heads = lax.all_to_all(
        to_groups(grad_attended), "fsdp", split_axis=3, concat_axis=2, tiled=True
    ).reshape(seq_count, pair_len, group_width)
    grad_query, grad_keys, grad_values = lax.map(
        attend_backward,
        (query_heads, key_all, value_all, grad_heads, summary, query_places, key_places),
    )
    kv_grads = jnp.concatenate([grad_keys, grad_values], axis=2).astype(jnp.bfloat16)
    kv_grads = kv_grads.reshape(seq_count, ctx_size, pair_len, 2 * group_width).transpose(1, 0, 2, 3)
    kv_part = lax.psum_scatter(
        kv_grads.reshape(ctx_size * seq_count * pair_len, 2 * group_width),
        CTX,
        scatter_dimension=0,
        tiled=True,
    ).reshape(seq_count, pair_len, 2 * group_width)
    key_part = kv_part[..., :group_width].astype(jnp.float32)
    value_part = kv_part[..., group_width:].astype(jnp.float32)
    key_grad_low = key_part.astype(jnp.bfloat16)
    value_grad_low = value_part.astype(jnp.bfloat16)
    query_back, key_back, value_back = (
        lax.all_to_all(
            for_sending(to_pairs(grad_query)), "fsdp", split_axis=2, concat_axis=3, tiled=True
        ),
        lax.all_to_all(
            for_sending(to_pairs(key_grad_low)), "fsdp", split_axis=2, concat_axis=3, tiled=True
        ),
        lax.all_to_all(
            for_sending(to_pairs(value_grad_low)), "fsdp", split_axis=2, concat_axis=3, tiled=True
        ),
    )
    grad_mixed = jnp.concatenate(
        [
            query_back.reshape(-1, model_width) * 0.125,
            key_back.reshape(-1, model_width),
            value_back.reshape(-1, model_width),
        ],
        axis=1,
    )
    qkv_grad = contract_first(core_major(normed_low, fsdp_size), grad_mixed)
    mixed_float = grad_mixed.astype(jnp.float32)
    query_bias_grad = jnp.sum(mixed_float[:, :model_width], axis=0)
    value_bias_grad = jnp.sum(mixed_float[:, 2 * model_width :], axis=0)
    grad_inputs, attn_gain_grad, attn_shift_grad = attn_norm_back(
        contract_last(grad_mixed, qkv_full)
    )
    in_grad = (grad_inputs + grad_middle).reshape(layer_in.shape)
    weight_totals = tuple(
        reduce_weight_grad(grad) for grad in (qkv_grad, out_weight_term, fc_grad, proj_grad)
    )
    vector_totals = []
    for grad in (
        attn_gain_grad,
        attn_shift_grad,
        query_bias_grad,
        value_bias_grad,
        out_bias_grad,
        mlp_gain_grad,
        mlp_shift_grad,
        fc_bias_grad,
        proj_bias_grad,
    ):
        share = lax.psum_scatter(grad.astype(jnp.bfloat16), "fsdp", scatter_dimension=0, tiled=True)
        piece = lax.psum_scatter(share, CTX, scatter_dimension=0, tiled=True)
        vector_totals.append(lax.all_gather(piece, CTX, axis=0, tiled=True).astype(jnp.float32))
    totals = weight_totals + tuple(vector_totals)
    return (
        layer_out,
        in_grad,
        totals[4],
        totals[5],
        totals[0],
        totals[6],
        totals[7],
        totals[1],
        totals[8],
        totals[9],
        totals[10],
        totals[2],
        totals[11],
        totals[3],
        totals[12],
    )


def solution(mesh):
    ctx_count, fsdp_count = mesh.devices.shape
    mesh = jax.sharding.Mesh(
        mesh.devices.reshape(ctx_count // 2, 2, fsdp_count), ("zc", "core", "fsdp")
    )
    placed = (
        P(None, CTX, None, "fsdp", None),
        P(None, CTX, None, "fsdp", None),
        P(),
        P("fsdp"),
        P("fsdp"),
        P("fsdp", None),
        P("fsdp"),
        P("fsdp"),
        P("fsdp", None),
        P("fsdp"),
        P("fsdp"),
        P("fsdp"),
        P("fsdp", None),
        P("fsdp"),
        P("fsdp", None),
        P("fsdp"),
    )
    return jax.shard_map(
        shards,
        mesh=mesh,
        in_specs=placed,
        out_specs=(
            P(None, CTX, None, "fsdp", None),
            P(None, CTX, None, "fsdp", None),
            P("fsdp"),
            P("fsdp"),
            P("fsdp", None),
            P("fsdp"),
            P("fsdp"),
            P("fsdp", None),
            P("fsdp"),
            P("fsdp"),
            P("fsdp"),
            P("fsdp", None),
            P("fsdp"),
            P("fsdp", None),
            P("fsdp"),
        ),
        check_vma=False,
    )
```

```python
import jax
import jax.numpy as jnp
from jax import lax
from jax.sharding import PartitionSpec as P

HD = 64


norm_eps = 1e-05
masked_score = -1e30


def for_sending(array):
    return jax.tree.map(lambda a: a.astype(jnp.bfloat16) if a.dtype == jnp.float32 else a, array)


def layer_norm(values, gain, shift):
    average = jnp.mean(values, axis=-1, keepdims=True)
    centred = values - average
    spread = jnp.mean(centred * centred, axis=-1, keepdims=True)
    return centred * lax.rsqrt(spread + norm_eps) * gain + shift


def gelu_tanh(values):
    return jax.nn.gelu(values, approximate=True)


def contract_last(left, right):
    return lax.dot_general(
        left, right, (((1,), (1,)), ((), ())), preferred_element_type=jnp.float32
    )


def contract_first(left, right):
    return lax.dot_general(
        left, right, (((0,), (0,)), ((), ())), preferred_element_type=jnp.float32
    )


def head_scores(query, keys, query_places, key_places):
    scores = contract_last(query, keys)
    return jnp.where(key_places[None, :] <= query_places[:, None], scores, masked_score)


def score_grads(query, keys, values, grad_out, summary, row_sum, query_places, key_places):
    scores = head_scores(query, keys, query_places, key_places)
    probs = jnp.exp(scores - summary[:, None])
    grad_probs = contract_last(grad_out, values)
    row_sum = jnp.sum(probs * grad_probs, axis=1)
    grad_scores = (probs * (grad_probs - row_sum[:, None])).astype(jnp.bfloat16)
    return (probs.astype(jnp.bfloat16), grad_scores, row_sum)


def attend_forward(items):
    query, keys, values, query_places, key_places = items
    outputs = []
    summaries = []
    for head_index in range(query.shape[1] // HD):
        columns = slice(head_index * HD, (head_index + 1) * HD)
        scores = head_scores(query[:, columns], keys[:, columns], query_places, key_places)
        row_peak = jnp.max(scores, axis=1, keepdims=True)
        raised = jnp.exp(scores - row_peak)
        row_total = jnp.sum(raised, axis=1, keepdims=True)
        weights = (raised / row_total).astype(jnp.bfloat16)
        outputs.append(
            jnp.dot(weights, values[:, columns], preferred_element_type=jnp.float32).astype(
                jnp.bfloat16
            )
        )
        summaries.append(row_peak[:, 0] + jnp.log(row_total[:, 0]))
    return (jnp.concatenate(outputs, axis=1), jnp.stack(summaries, axis=1))


def attend_backward(items):
    query, keys, values, grad_out, summary, query_places, key_places = items
    query_parts, key_parts, value_parts = ([], [], [])
    for head_index in range(query.shape[1] // HD):
        columns = slice(head_index * HD, (head_index + 1) * HD)
        probs_low, grad_scores, row_sum = score_grads(
            query[:, columns],
            keys[:, columns],
            values[:, columns],
            grad_out[:, columns],
            summary[:, head_index],
            None,
            query_places,
            key_places,
        )
        query_parts.append(
            jnp.dot(grad_scores, keys[:, columns], preferred_element_type=jnp.float32).astype(
                jnp.bfloat16
            )
        )
        key_parts.append(contract_first(grad_scores, query[:, columns]))
        value_parts.append(contract_first(probs_low, grad_out[:, columns]))
    return (
        jnp.concatenate(query_parts, axis=1),
        jnp.concatenate(key_parts, axis=1),
        jnp.concatenate(value_parts, axis=1),
    )


CTX = ("zc", "core")


def gather_weight(shard):
    half = shard.shape[0] // 2
    piece = lax.dynamic_slice_in_dim(shard, lax.axis_index("core") * half, half, 0)
    fsdp_size = lax.axis_size("fsdp")
    pieces = lax.all_to_all(
        jnp.broadcast_to(piece[None], (fsdp_size,) + piece.shape),
        "fsdp",
        split_axis=0,
        concat_axis=0,
        tiled=True,
    )
    whole = lax.all_gather(pieces, "core", axis=1, tiled=True)
    return whole.reshape(-1, shard.shape[1])


def core_major(rows, fsdp_size):
    count, width = rows.shape
    return rows.reshape(count, fsdp_size, 2, width // (2 * fsdp_size)).transpose(0, 2, 1, 3).reshape(
        count, width
    )


def reduce_weight_grad(grad):
    grad = lax.psum_scatter(grad.astype(jnp.bfloat16), "core", scatter_dimension=0, tiled=True)
    fsdp_size = lax.axis_size("fsdp")
    blocks = lax.all_to_all(
        grad.reshape((fsdp_size, -1) + grad.shape[1:]), "fsdp", split_axis=0, concat_axis=0, tiled=True
    )
    grad = jnp.sum(blocks.astype(jnp.float32), axis=0).astype(jnp.bfloat16)
    grad = lax.psum_scatter(grad, "zc", scatter_dimension=0, tiled=True)
    grad = lax.all_gather(grad, "zc", axis=0, tiled=True)
    grad = lax.all_gather(grad, "core", axis=0, tiled=True)
    return grad.astype(jnp.float32)


def shards(
    layer_in,
    out_grad,
    block_pairs,
    attn_gain,
    attn_shift,
    qkv_weight,
    query_bias,
    value_bias,
    out_weight,
    out_bias,
    mlp_gain,
    mlp_shift,
    fc_weight,
    fc_bias,
    proj_weight,
    proj_bias,
):
    fsdp_size = lax.axis_size("fsdp")
    ctx_size = lax.axis_size("zc") * lax.axis_size("core")
    seq_count = layer_in.shape[0]
    half_rows = layer_in.shape[3]
    model_width = layer_in.shape[4]
    block_len = half_rows * fsdp_size
    pair_len = 2 * block_len
    group_width = model_width // fsdp_size
    gathered = (
        gather_weight(qkv_weight),
        gather_weight(out_weight),
        gather_weight(fc_weight),
        gather_weight(proj_weight),
        lax.all_gather(attn_gain, "fsdp", axis=0, tiled=True),
        lax.all_gather(attn_shift, "fsdp", axis=0, tiled=True),
        lax.all_gather(query_bias, "fsdp", axis=0, tiled=True),
        lax.all_gather(value_bias, "fsdp", axis=0, tiled=True),
        lax.all_gather(out_bias, "fsdp", axis=0, tiled=True),
        lax.all_gather(mlp_gain, "fsdp", axis=0, tiled=True),
        lax.all_gather(mlp_shift, "fsdp", axis=0, tiled=True),
        lax.all_gather(fc_bias, "fsdp", axis=0, tiled=True),
        lax.all_gather(proj_bias, "fsdp", axis=0, tiled=True),
    )
    qkv_full, out_full, fc_full, proj_full = (gathered[0], gathered[1], gathered[2], gathered[3])
    vectors = [piece.astype(jnp.float32) for piece in gathered[4:]]
    (
        gain_attn,
        shift_attn,
        bias_query,
        bias_value,
        bias_out,
        gain_mlp,
        shift_mlp,
        bias_fc,
        bias_proj,
    ) = vectors
    halves = jnp.stack([block_pairs, 2 * ctx_size - 1 - block_pairs], axis=2)
    key_places = (halves[..., None] * block_len + jnp.arange(block_len, dtype=jnp.int32)).reshape(
        seq_count, ctx_size, pair_len
    )
    query_places = lax.dynamic_slice_in_dim(key_places, lax.axis_index(CTX), 1, 1).reshape(
        seq_count, pair_len
    )
    key_places = key_places.reshape(seq_count, ctx_size * pair_len)
    inputs = layer_in.reshape(-1, model_width).astype(jnp.float32)
    normed, attn_norm_back = jax.vjp(layer_norm, inputs, gain_attn, shift_attn)
    normed_low = normed.astype(jnp.bfloat16)
    mixed = jnp.dot(normed_low, qkv_full, preferred_element_type=jnp.float32)
    query = ((mixed[:, :model_width] + bias_query) * 0.125).astype(jnp.bfloat16)
    keys = mixed[:, model_width : 2 * model_width].astype(jnp.bfloat16)
    values = (mixed[:, 2 * model_width :] + bias_value).astype(jnp.bfloat16)

    def to_groups(array):
        return array.reshape(seq_count, 2, half_rows, fsdp_size, group_width)

    def to_pairs(array):
        return array.reshape(seq_count, 2, block_len, 1, group_width)

    query_heads, key_heads, value_heads = (
        lax.all_to_all(to_groups(query), "fsdp", split_axis=3, concat_axis=2, tiled=True),
        lax.all_to_all(to_groups(keys), "fsdp", split_axis=3, concat_axis=2, tiled=True),
        lax.all_to_all(to_groups(values), "fsdp", split_axis=3, concat_axis=2, tiled=True),
    )
    query_heads = query_heads.reshape(seq_count, pair_len, group_width)
    own_keys = key_heads.reshape(seq_count, pair_len, group_width)
    own_values = value_heads.reshape(seq_count, pair_len, group_width)
    key_all, value_all = (
        lax.all_to_all(
            jnp.broadcast_to(own[None], (ctx_size,) + own.shape), CTX, split_axis=0, concat_axis=0, tiled=True
        ).transpose(1, 0, 2, 3)
        for own in (own_keys, own_values)
    )
    key_all = key_all.reshape(seq_count, -1, group_width)
    value_all = value_all.reshape(seq_count, -1, group_width)
    attended, summary = lax.map(
        attend_forward, (query_heads, key_all, value_all, query_places, key_places)
    )
    attended_rows = lax.all_to_all(
        for_sending(to_pairs(attended)), "fsdp", split_axis=2, concat_axis=3, tiled=True
    ).reshape(-1, model_width)
    branch = jnp.dot(attended_rows, out_full, preferred_element_type=jnp.float32) + bias_out
    middle = inputs + branch
    normed_mlp, mlp_norm_back = jax.vjp(layer_norm, middle, gain_mlp, shift_mlp)
    mlp_low = normed_mlp.astype(jnp.bfloat16)
    hidden = jnp.dot(mlp_low, fc_full, preferred_element_type=jnp.float32) + bias_fc
    activated, gelu_back = jax.vjp(gelu_tanh, hidden)
    activated_low = activated.astype(jnp.bfloat16)
    result = (
        middle + jnp.dot(activated_low, proj_full, preferred_element_type=jnp.float32) + bias_proj
    )
    layer_out = result.astype(jnp.bfloat16).reshape(layer_in.shape)
    grad_rows = out_grad.reshape(-1, model_width)
    grad_result = grad_rows.astype(jnp.float32)
    proj_grad = contract_first(core_major(activated_low, fsdp_size), grad_rows)
    proj_bias_grad = jnp.sum(grad_result, axis=0)
    grad_activated = contract_last(grad_rows, proj_full)
    grad_hidden = gelu_back(grad_activated)[0].astype(jnp.bfloat16)
    fc_grad = contract_first(core_major(mlp_low, fsdp_size), grad_hidden)
    fc_bias_grad = jnp.sum(grad_hidden.astype(jnp.float32), axis=0)
    grad_middle, mlp_gain_grad, mlp_shift_grad = mlp_norm_back(contract_last(grad_hidden, fc_full))
    grad_middle = grad_middle + grad_result
    grad_branch = grad_middle.astype(jnp.bfloat16)
    out_weight_term = contract_first(core_major(attended_rows, fsdp_size), grad_branch)
    out_bias_grad = jnp.sum(grad_branch.astype(jnp.float32), axis=0)
    grad_attended = contract_last(grad_branch, out_full).astype(jnp.bfloat16)
    grad_heads = lax.all_to_all(
        to_groups(grad_attended), "fsdp", split_axis=3, concat_axis=2, tiled=True
    ).reshape(seq_count, pair_len, group_width)
    grad_query, grad_keys, grad_values = lax.map(
        attend_backward,
        (query_heads, key_all, value_all, grad_heads, summary, query_places, key_places),
    )
    kv_grads = jnp.concatenate([grad_keys, grad_values], axis=2).astype(jnp.bfloat16)
    kv_grads = kv_grads.reshape(seq_count, ctx_size, pair_len, 2 * group_width).transpose(1, 0, 2, 3)
    kv_part = jnp.sum(
        lax.all_to_all(kv_grads, CTX, split_axis=0, concat_axis=0, tiled=True).astype(jnp.float32),
        axis=0,
    ).astype(jnp.bfloat16)
    key_part = kv_part[..., :group_width].astype(jnp.float32)
    value_part = kv_part[..., group_width:].astype(jnp.float32)
    key_grad_low = key_part.astype(jnp.bfloat16)
    value_grad_low = value_part.astype(jnp.bfloat16)
    query_back, key_back, value_back = (
        lax.all_to_all(
            for_sending(to_pairs(grad_query)), "fsdp", split_axis=2, concat_axis=3, tiled=True
        ),
        lax.all_to_all(
            for_sending(to_pairs(key_grad_low)), "fsdp", split_axis=2, concat_axis=3, tiled=True
        ),
        lax.all_to_all(
            for_sending(to_pairs(value_grad_low)), "fsdp", split_axis=2, concat_axis=3, tiled=True
        ),
    )
    grad_mixed = jnp.concatenate(
        [
            query_back.reshape(-1, model_width) * 0.125,
            key_back.reshape(-1, model_width),
            value_back.reshape(-1, model_width),
        ],
        axis=1,
    )
    qkv_grad = contract_first(core_major(normed_low, fsdp_size), grad_mixed)
    mixed_float = grad_mixed.astype(jnp.float32)
    query_bias_grad = jnp.sum(mixed_float[:, :model_width], axis=0)
    value_bias_grad = jnp.sum(mixed_float[:, 2 * model_width :], axis=0)
    grad_inputs, attn_gain_grad, attn_shift_grad = attn_norm_back(
        contract_last(grad_mixed, qkv_full)
    )
    in_grad = (grad_inputs + grad_middle).reshape(layer_in.shape)
    weight_totals = tuple(
        reduce_weight_grad(grad) for grad in (qkv_grad, out_weight_term, fc_grad, proj_grad)
    )
    vector_totals = []
    for grad in (
        attn_gain_grad,
        attn_shift_grad,
        query_bias_grad,
        value_bias_grad,
        out_bias_grad,
        mlp_gain_grad,
        mlp_shift_grad,
        fc_bias_grad,
        proj_bias_grad,
    ):
        share = lax.psum_scatter(grad.astype(jnp.bfloat16), "fsdp", scatter_dimension=0, tiled=True)
        piece = lax.psum_scatter(share, CTX, scatter_dimension=0, tiled=True)
        vector_totals.append(lax.all_gather(piece, CTX, axis=0, tiled=True).astype(jnp.float32))
    totals = weight_totals + tuple(vector_totals)
    return (
        layer_out,
        in_grad,
        totals[4],
        totals[5],
        totals[0],
        totals[6],
        totals[7],
        totals[1],
        totals[8],
        totals[9],
        totals[10],
        totals[2],
        totals[11],
        totals[3],
        totals[12],
    )


def solution(mesh):
    ctx_count, fsdp_count = mesh.devices.shape
    mesh = jax.sharding.Mesh(
        mesh.devices.reshape(ctx_count // 2, 2, fsdp_count), ("zc", "core", "fsdp")
    )
    placed = (
        P(None, CTX, None, "fsdp", None),
        P(None, CTX, None, "fsdp", None),
        P(),
        P("fsdp"),
        P("fsdp"),
        P("fsdp", None),
        P("fsdp"),
        P("fsdp"),
        P("fsdp", None),
        P("fsdp"),
        P("fsdp"),
        P("fsdp"),
        P("fsdp", None),
        P("fsdp"),
        P("fsdp", None),
        P("fsdp"),
    )
    return jax.shard_map(
        shards,
        mesh=mesh,
        in_specs=placed,
        out_specs=(
            P(None, CTX, None, "fsdp", None),
            P(None, CTX, None, "fsdp", None),
            P("fsdp"),
            P("fsdp"),
            P("fsdp", None),
            P("fsdp"),
            P("fsdp"),
            P("fsdp", None),
            P("fsdp"),
            P("fsdp"),
            P("fsdp"),
            P("fsdp", None),
            P("fsdp"),
            P("fsdp", None),
            P("fsdp"),
        ),
        check_vma=False,
    )
```

```python
import jax
import jax.numpy as jnp
from jax import lax
from jax.sharding import PartitionSpec as P

HD = 64


norm_eps = 1e-05
masked_score = -1e30


def for_sending(array):
    return jax.tree.map(lambda a: a.astype(jnp.bfloat16) if a.dtype == jnp.float32 else a, array)


def layer_norm(values, gain, shift):
    average = jnp.mean(values, axis=-1, keepdims=True)
    centred = values - average
    spread = jnp.mean(centred * centred, axis=-1, keepdims=True)
    return centred * lax.rsqrt(spread + norm_eps) * gain + shift


def gelu_tanh(values):
    return jax.nn.gelu(values, approximate=True)


def contract_last(left, right):
    return lax.dot_general(
        left, right, (((1,), (1,)), ((), ())), preferred_element_type=jnp.float32
    )


def contract_first(left, right):
    return lax.dot_general(
        left, right, (((0,), (0,)), ((), ())), preferred_element_type=jnp.float32
    )


def head_scores(query, keys, query_places, key_places):
    scores = contract_last(query, keys)
    return jnp.where(key_places[None, :] <= query_places[:, None], scores, masked_score)


def score_grads(query, keys, values, grad_out, summary, row_sum, query_places, key_places):
    scores = head_scores(query, keys, query_places, key_places)
    probs = jnp.exp(scores - summary[:, None])
    grad_probs = contract_last(grad_out, values)
    row_sum = jnp.sum(probs * grad_probs, axis=1)
    grad_scores = (probs * (grad_probs - row_sum[:, None])).astype(jnp.bfloat16)
    return (probs.astype(jnp.bfloat16), grad_scores, row_sum)


def attend_forward(items):
    query, keys, values, query_places, key_places = items
    outputs = []
    summaries = []
    for head_index in range(query.shape[1] // HD):
        columns = slice(head_index * HD, (head_index + 1) * HD)
        scores = head_scores(query[:, columns], keys[:, columns], query_places, key_places)
        row_peak = jnp.max(scores, axis=1, keepdims=True)
        raised = jnp.exp(scores - row_peak)
        row_total = jnp.sum(raised, axis=1, keepdims=True)
        weights = (raised / row_total).astype(jnp.bfloat16)
        outputs.append(
            jnp.dot(weights, values[:, columns], preferred_element_type=jnp.float32).astype(
                jnp.bfloat16
            )
        )
        summaries.append(row_peak[:, 0] + jnp.log(row_total[:, 0]))
    return (jnp.concatenate(outputs, axis=1), jnp.stack(summaries, axis=1))


def attend_backward(items):
    query, keys, values, grad_out, summary, query_places, key_places = items
    query_parts, key_parts, value_parts = ([], [], [])
    for head_index in range(query.shape[1] // HD):
        columns = slice(head_index * HD, (head_index + 1) * HD)
        probs_low, grad_scores, row_sum = score_grads(
            query[:, columns],
            keys[:, columns],
            values[:, columns],
            grad_out[:, columns],
            summary[:, head_index],
            None,
            query_places,
            key_places,
        )
        query_parts.append(
            jnp.dot(grad_scores, keys[:, columns], preferred_element_type=jnp.float32).astype(
                jnp.bfloat16
            )
        )
        key_parts.append(contract_first(grad_scores, query[:, columns]))
        value_parts.append(contract_first(probs_low, grad_out[:, columns]))
    return (
        jnp.concatenate(query_parts, axis=1),
        jnp.concatenate(key_parts, axis=1),
        jnp.concatenate(value_parts, axis=1),
    )


CTX = ("zc", "core")


def gather_weight(shard):
    half = shard.shape[0] // 2
    piece = lax.dynamic_slice_in_dim(shard, lax.axis_index("core") * half, half, 0)
    fsdp_size = lax.axis_size("fsdp")
    pieces = lax.all_to_all(
        jnp.broadcast_to(piece[None], (fsdp_size,) + piece.shape),
        "fsdp",
        split_axis=0,
        concat_axis=0,
        tiled=True,
    )
    whole = lax.all_gather(pieces, "core", axis=1, tiled=True)
    return whole.reshape(-1, shard.shape[1])


def core_major(rows, fsdp_size):
    count, width = rows.shape
    return rows.reshape(count, fsdp_size, 2, width // (2 * fsdp_size)).transpose(0, 2, 1, 3).reshape(
        count, width
    )


def reduce_weight_grad(grad):
    grad = lax.psum_scatter(grad.astype(jnp.bfloat16), "core", scatter_dimension=0, tiled=True)
    fsdp_size = lax.axis_size("fsdp")
    blocks = lax.all_to_all(
        grad.reshape((fsdp_size, -1) + grad.shape[1:]), "fsdp", split_axis=0, concat_axis=0, tiled=True
    )
    grad = jnp.sum(blocks.astype(jnp.float32), axis=0).astype(jnp.bfloat16)
    grad = lax.psum_scatter(grad, "zc", scatter_dimension=0, tiled=True)
    grad = lax.all_gather(grad, "zc", axis=0, tiled=True)
    grad = lax.all_gather(grad, "core", axis=0, tiled=True)
    return grad.astype(jnp.float32)


def shards(
    layer_in,
    out_grad,
    block_pairs,
    attn_gain,
    attn_shift,
    qkv_weight,
    query_bias,
    value_bias,
    out_weight,
    out_bias,
    mlp_gain,
    mlp_shift,
    fc_weight,
    fc_bias,
    proj_weight,
    proj_bias,
):
    fsdp_size = lax.axis_size("fsdp")
    ctx_size = lax.axis_size("zc") * lax.axis_size("core")
    seq_count = layer_in.shape[0]
    half_rows = layer_in.shape[3]
    model_width = layer_in.shape[4]
    block_len = half_rows * fsdp_size
    pair_len = 2 * block_len
    group_width = model_width // fsdp_size
    gathered = (
        gather_weight(qkv_weight),
        gather_weight(out_weight),
        gather_weight(fc_weight),
        gather_weight(proj_weight),
        lax.all_gather(attn_gain, "fsdp", axis=0, tiled=True),
        lax.all_gather(attn_shift, "fsdp", axis=0, tiled=True),
        lax.all_gather(query_bias, "fsdp", axis=0, tiled=True),
        lax.all_gather(value_bias, "fsdp", axis=0, tiled=True),
        lax.all_gather(out_bias, "fsdp", axis=0, tiled=True),
        lax.all_gather(mlp_gain, "fsdp", axis=0, tiled=True),
        lax.all_gather(mlp_shift, "fsdp", axis=0, tiled=True),
        lax.all_gather(fc_bias, "fsdp", axis=0, tiled=True),
        lax.all_gather(proj_bias, "fsdp", axis=0, tiled=True),
    )
    qkv_full, out_full, fc_full, proj_full = (gathered[0], gathered[1], gathered[2], gathered[3])
    vectors = [piece.astype(jnp.float32) for piece in gathered[4:]]
    (
        gain_attn,
        shift_attn,
        bias_query,
        bias_value,
        bias_out,
        gain_mlp,
        shift_mlp,
        bias_fc,
        bias_proj,
    ) = vectors
    halves = jnp.stack([block_pairs, 2 * ctx_size - 1 - block_pairs], axis=2)
    key_places = (halves[..., None] * block_len + jnp.arange(block_len, dtype=jnp.int32)).reshape(
        seq_count, ctx_size, pair_len
    )
    query_places = lax.dynamic_slice_in_dim(key_places, lax.axis_index(CTX), 1, 1).reshape(
        seq_count, pair_len
    )
    key_places = key_places.reshape(seq_count, ctx_size * pair_len)
    inputs = layer_in.reshape(-1, model_width).astype(jnp.float32)
    normed, attn_norm_back = jax.vjp(layer_norm, inputs, gain_attn, shift_attn)
    normed_low = normed.astype(jnp.bfloat16)
    mixed = jnp.dot(normed_low, qkv_full, preferred_element_type=jnp.float32)
    query = ((mixed[:, :model_width] + bias_query) * 0.125).astype(jnp.bfloat16)
    keys = mixed[:, model_width : 2 * model_width].astype(jnp.bfloat16)
    values = (mixed[:, 2 * model_width :] + bias_value).astype(jnp.bfloat16)

    def to_groups(array):
        return array.reshape(seq_count, 2, half_rows, fsdp_size, group_width)

    def to_pairs(array):
        return array.reshape(seq_count, 2, block_len, 1, group_width)

    query_heads, key_heads, value_heads = (
        lax.all_to_all(to_groups(query), "fsdp", split_axis=3, concat_axis=2, tiled=True),
        lax.all_to_all(to_groups(keys), "fsdp", split_axis=3, concat_axis=2, tiled=True),
        lax.all_to_all(to_groups(values), "fsdp", split_axis=3, concat_axis=2, tiled=True),
    )
    query_heads = query_heads.reshape(seq_count, pair_len, group_width)
    own_keys = key_heads.reshape(seq_count, pair_len, group_width)
    own_values = value_heads.reshape(seq_count, pair_len, group_width)
    key_all, value_all = (
        lax.all_gather(
            own_keys.reshape(seq_count, 1, pair_len, group_width), CTX, axis=1, tiled=True
        ),
        lax.all_gather(
            own_values.reshape(seq_count, 1, pair_len, group_width), CTX, axis=1, tiled=True
        ),
    )
    key_all = key_all.reshape(seq_count, -1, group_width)
    value_all = value_all.reshape(seq_count, -1, group_width)
    attended, summary = lax.map(
        attend_forward, (query_heads, key_all, value_all, query_places, key_places)
    )
    attended_rows = lax.all_to_all(
        for_sending(to_pairs(attended)), "fsdp", split_axis=2, concat_axis=3, tiled=True
    ).reshape(-1, model_width)
    branch = jnp.dot(attended_rows, out_full, preferred_element_type=jnp.float32) + bias_out
    middle = inputs + branch
    normed_mlp, mlp_norm_back = jax.vjp(layer_norm, middle, gain_mlp, shift_mlp)
    mlp_low = normed_mlp.astype(jnp.bfloat16)
    hidden = jnp.dot(mlp_low, fc_full, preferred_element_type=jnp.float32) + bias_fc
    activated, gelu_back = jax.vjp(gelu_tanh, hidden)
    activated_low = activated.astype(jnp.bfloat16)
    result = (
        middle + jnp.dot(activated_low, proj_full, preferred_element_type=jnp.float32) + bias_proj
    )
    layer_out = result.astype(jnp.bfloat16).reshape(layer_in.shape)
    grad_rows = out_grad.reshape(-1, model_width)
    grad_result = grad_rows.astype(jnp.float32)
    proj_grad = contract_first(core_major(activated_low, fsdp_size), grad_rows)
    proj_bias_grad = jnp.sum(grad_result, axis=0)
    grad_activated = contract_last(grad_rows, proj_full)
    grad_hidden = gelu_back(grad_activated)[0].astype(jnp.bfloat16)
    fc_grad = contract_first(core_major(mlp_low, fsdp_size), grad_hidden)
    fc_bias_grad = jnp.sum(grad_hidden.astype(jnp.float32), axis=0)
    grad_middle, mlp_gain_grad, mlp_shift_grad = mlp_norm_back(contract_last(grad_hidden, fc_full))
    grad_middle = grad_middle + grad_result
    grad_branch = grad_middle.astype(jnp.bfloat16)
    out_weight_term = contract_first(core_major(attended_rows, fsdp_size), grad_branch)
    out_bias_grad = jnp.sum(grad_branch.astype(jnp.float32), axis=0)
    grad_attended = contract_last(grad_branch, out_full).astype(jnp.bfloat16)
    grad_heads = lax.all_to_all(
        to_groups(grad_attended), "fsdp", split_axis=3, concat_axis=2, tiled=True
    ).reshape(seq_count, pair_len, group_width)
    grad_query, grad_keys, grad_values = lax.map(
        attend_backward,
        (query_heads, key_all, value_all, grad_heads, summary, query_places, key_places),
    )
    kv_grads = jnp.concatenate([grad_keys, grad_values], axis=2).astype(jnp.bfloat16)
    kv_grads = kv_grads.reshape(seq_count, ctx_size, pair_len, 2 * group_width).transpose(1, 0, 2, 3)
    kv_part = lax.psum_scatter(
        kv_grads.reshape(ctx_size * seq_count * pair_len, 2 * group_width),
        CTX,
        scatter_dimension=0,
        tiled=True,
    ).reshape(seq_count, pair_len, 2 * group_width)
    key_part = kv_part[..., :group_width].astype(jnp.float32)
    value_part = kv_part[..., group_width:].astype(jnp.float32)
    key_grad_low = key_part.astype(jnp.bfloat16)
    value_grad_low = value_part.astype(jnp.bfloat16)
    query_back, key_back, value_back = (
        lax.all_to_all(
            for_sending(to_pairs(grad_query)), "fsdp", split_axis=2, concat_axis=3, tiled=True
        ),
        lax.all_to_all(
            for_sending(to_pairs(key_grad_low)), "fsdp", split_axis=2, concat_axis=3, tiled=True
        ),
        lax.all_to_all(
            for_sending(to_pairs(value_grad_low)), "fsdp", split_axis=2, concat_axis=3, tiled=True
        ),
    )
    grad_mixed = jnp.concatenate(
        [
            query_back.reshape(-1, model_width) * 0.125,
            key_back.reshape(-1, model_width),
            value_back.reshape(-1, model_width),
        ],
        axis=1,
    )
    qkv_grad = contract_first(core_major(normed_low, fsdp_size), grad_mixed)
    mixed_float = grad_mixed.astype(jnp.float32)
    query_bias_grad = jnp.sum(mixed_float[:, :model_width], axis=0)
    value_bias_grad = jnp.sum(mixed_float[:, 2 * model_width :], axis=0)
    grad_inputs, attn_gain_grad, attn_shift_grad = attn_norm_back(
        contract_last(grad_mixed, qkv_full)
    )
    in_grad = (grad_inputs + grad_middle).reshape(layer_in.shape)
    weight_totals = tuple(
        reduce_weight_grad(grad) for grad in (qkv_grad, out_weight_term, fc_grad, proj_grad)
    )
    vector_grads = (
        attn_gain_grad,
        attn_shift_grad,
        query_bias_grad,
        value_bias_grad,
        out_bias_grad,
        mlp_gain_grad,
        mlp_shift_grad,
        fc_bias_grad,
        proj_bias_grad,
    )
    packed = jnp.concatenate(
        [grad.astype(jnp.bfloat16).reshape(fsdp_size, -1) for grad in vector_grads], axis=1
    )
    packed = lax.psum_scatter(packed, "fsdp", scatter_dimension=0, tiled=True).reshape(-1)
    packed = lax.psum_scatter(packed, CTX, scatter_dimension=0, tiled=True)
    packed = lax.all_gather(packed, CTX, axis=0, tiled=True).astype(jnp.float32)
    vector_totals = []
    offset = 0
    for grad in vector_grads:
        width = grad.shape[0] // fsdp_size
        vector_totals.append(packed[offset : offset + width])
        offset += width
    totals = weight_totals + tuple(vector_totals)
    return (
        layer_out,
        in_grad,
        totals[4],
        totals[5],
        totals[0],
        totals[6],
        totals[7],
        totals[1],
        totals[8],
        totals[9],
        totals[10],
        totals[2],
        totals[11],
        totals[3],
        totals[12],
    )


def solution(mesh):
    ctx_count, fsdp_count = mesh.devices.shape
    mesh = jax.sharding.Mesh(
        mesh.devices.reshape(ctx_count // 2, 2, fsdp_count), ("zc", "core", "fsdp")
    )
    placed = (
        P(None, CTX, None, "fsdp", None),
        P(None, CTX, None, "fsdp", None),
        P(),
        P("fsdp"),
        P("fsdp"),
        P("fsdp", None),
        P("fsdp"),
        P("fsdp"),
        P("fsdp", None),
        P("fsdp"),
        P("fsdp"),
        P("fsdp"),
        P("fsdp", None),
        P("fsdp"),
        P("fsdp", None),
        P("fsdp"),
    )
    return jax.shard_map(
        shards,
        mesh=mesh,
        in_specs=placed,
        out_specs=(
            P(None, CTX, None, "fsdp", None),
            P(None, CTX, None, "fsdp", None),
            P("fsdp"),
            P("fsdp"),
            P("fsdp", None),
            P("fsdp"),
            P("fsdp"),
            P("fsdp", None),
            P("fsdp"),
            P("fsdp"),
            P("fsdp"),
            P("fsdp", None),
            P("fsdp"),
            P("fsdp", None),
            P("fsdp"),
        ),
        check_vma=False,
    )
```

```python
import jax
import jax.numpy as jnp
from jax import lax
from jax.sharding import PartitionSpec as P

HD = 64


norm_eps = 1e-05
masked_score = -1e30


def for_sending(array):
    return jax.tree.map(lambda a: a.astype(jnp.bfloat16) if a.dtype == jnp.float32 else a, array)


def layer_norm(values, gain, shift):
    average = jnp.mean(values, axis=-1, keepdims=True)
    centred = values - average
    spread = jnp.mean(centred * centred, axis=-1, keepdims=True)
    return centred * lax.rsqrt(spread + norm_eps) * gain + shift


def gelu_tanh(values):
    return jax.nn.gelu(values, approximate=True)


def contract_last(left, right):
    return lax.dot_general(
        left, right, (((1,), (1,)), ((), ())), preferred_element_type=jnp.float32
    )


def contract_first(left, right):
    return lax.dot_general(
        left, right, (((0,), (0,)), ((), ())), preferred_element_type=jnp.float32
    )


def head_scores(query, keys, query_places, key_places):
    scores = contract_last(query, keys)
    return jnp.where(key_places[None, :] <= query_places[:, None], scores, masked_score)


def score_grads(query, keys, values, grad_out, summary, row_sum, query_places, key_places):
    scores = head_scores(query, keys, query_places, key_places)
    probs = jnp.exp(scores - summary[:, None])
    grad_probs = contract_last(grad_out, values)
    row_sum = jnp.sum(probs * grad_probs, axis=1)
    grad_scores = (probs * (grad_probs - row_sum[:, None])).astype(jnp.bfloat16)
    return (probs.astype(jnp.bfloat16), grad_scores, row_sum)


def attend_forward(items):
    query, keys, values, query_places, key_places = items
    outputs = []
    summaries = []
    for head_index in range(query.shape[1] // HD):
        columns = slice(head_index * HD, (head_index + 1) * HD)
        scores = head_scores(query[:, columns], keys[:, columns], query_places, key_places)
        row_peak = jnp.max(scores, axis=1, keepdims=True)
        raised = jnp.exp(scores - row_peak)
        row_total = jnp.sum(raised, axis=1, keepdims=True)
        weights = (raised / row_total).astype(jnp.bfloat16)
        outputs.append(
            jnp.dot(weights, values[:, columns], preferred_element_type=jnp.float32).astype(
                jnp.bfloat16
            )
        )
        summaries.append(row_peak[:, 0] + jnp.log(row_total[:, 0]))
    return (jnp.concatenate(outputs, axis=1), jnp.stack(summaries, axis=1))


def attend_backward(items):
    query, keys, values, grad_out, summary, query_places, key_places = items
    query_parts, key_parts, value_parts = ([], [], [])
    for head_index in range(query.shape[1] // HD):
        columns = slice(head_index * HD, (head_index + 1) * HD)
        probs_low, grad_scores, row_sum = score_grads(
            query[:, columns],
            keys[:, columns],
            values[:, columns],
            grad_out[:, columns],
            summary[:, head_index],
            None,
            query_places,
            key_places,
        )
        query_parts.append(
            jnp.dot(grad_scores, keys[:, columns], preferred_element_type=jnp.float32).astype(
                jnp.bfloat16
            )
        )
        key_parts.append(contract_first(grad_scores, query[:, columns]))
        value_parts.append(contract_first(probs_low, grad_out[:, columns]))
    return (
        jnp.concatenate(query_parts, axis=1),
        jnp.concatenate(key_parts, axis=1),
        jnp.concatenate(value_parts, axis=1),
    )


CTX = ("zc", "core")


def gather_weight(shard):
    half = shard.shape[0] // 2
    piece = lax.dynamic_slice_in_dim(shard, lax.axis_index("core") * half, half, 0)
    fsdp_size = lax.axis_size("fsdp")
    pieces = lax.all_to_all(
        jnp.broadcast_to(piece[None], (fsdp_size,) + piece.shape),
        "fsdp",
        split_axis=0,
        concat_axis=0,
        tiled=True,
    )
    whole = lax.all_gather(pieces, "core", axis=1, tiled=True)
    return whole.reshape(-1, shard.shape[1])


def core_major(rows, fsdp_size):
    count, width = rows.shape
    return rows.reshape(count, fsdp_size, 2, width // (2 * fsdp_size)).transpose(0, 2, 1, 3).reshape(
        count, width
    )


def reduce_weight_grad(grad):
    grad = lax.psum_scatter(grad.astype(jnp.bfloat16), "core", scatter_dimension=0, tiled=True)
    fsdp_size = lax.axis_size("fsdp")
    blocks = lax.all_to_all(
        grad.reshape((fsdp_size, -1) + grad.shape[1:]), "fsdp", split_axis=0, concat_axis=0, tiled=True
    )
    return jnp.sum(blocks.astype(jnp.float32), axis=0).astype(jnp.bfloat16)


def finish_weight_grads(grads):
    packed = jnp.concatenate([grad.reshape(-1, 512) for grad in grads])
    packed = lax.psum_scatter(packed, "zc", scatter_dimension=0, tiled=True)
    packed = lax.all_gather(packed, "zc", axis=0, tiled=True).reshape(-1)
    packed = lax.all_gather(packed, "core", axis=0, tiled=False).astype(jnp.float32)
    totals = []
    offset = 0
    for grad in grads:
        size = grad.size
        totals.append(packed[:, offset : offset + size].reshape((-1,) + grad.shape[1:]))
        offset += size
    return tuple(totals)


def shards(
    layer_in,
    out_grad,
    block_pairs,
    attn_gain,
    attn_shift,
    qkv_weight,
    query_bias,
    value_bias,
    out_weight,
    out_bias,
    mlp_gain,
    mlp_shift,
    fc_weight,
    fc_bias,
    proj_weight,
    proj_bias,
):
    fsdp_size = lax.axis_size("fsdp")
    ctx_size = lax.axis_size("zc") * lax.axis_size("core")
    seq_count = layer_in.shape[0]
    half_rows = layer_in.shape[3]
    model_width = layer_in.shape[4]
    block_len = half_rows * fsdp_size
    pair_len = 2 * block_len
    group_width = model_width // fsdp_size
    gathered = (
        gather_weight(qkv_weight),
        gather_weight(out_weight),
        gather_weight(fc_weight),
        gather_weight(proj_weight),
        lax.all_gather(attn_gain, "fsdp", axis=0, tiled=True),
        lax.all_gather(attn_shift, "fsdp", axis=0, tiled=True),
        lax.all_gather(query_bias, "fsdp", axis=0, tiled=True),
        lax.all_gather(value_bias, "fsdp", axis=0, tiled=True),
        lax.all_gather(out_bias, "fsdp", axis=0, tiled=True),
        lax.all_gather(mlp_gain, "fsdp", axis=0, tiled=True),
        lax.all_gather(mlp_shift, "fsdp", axis=0, tiled=True),
        lax.all_gather(fc_bias, "fsdp", axis=0, tiled=True),
        lax.all_gather(proj_bias, "fsdp", axis=0, tiled=True),
    )
    qkv_full, out_full, fc_full, proj_full = (gathered[0], gathered[1], gathered[2], gathered[3])
    vectors = [piece.astype(jnp.float32) for piece in gathered[4:]]
    (
        gain_attn,
        shift_attn,
        bias_query,
        bias_value,
        bias_out,
        gain_mlp,
        shift_mlp,
        bias_fc,
        bias_proj,
    ) = vectors
    halves = jnp.stack([block_pairs, 2 * ctx_size - 1 - block_pairs], axis=2)
    key_places = (halves[..., None] * block_len + jnp.arange(block_len, dtype=jnp.int32)).reshape(
        seq_count, ctx_size, pair_len
    )
    query_places = lax.dynamic_slice_in_dim(key_places, lax.axis_index(CTX), 1, 1).reshape(
        seq_count, pair_len
    )
    key_places = key_places.reshape(seq_count, ctx_size * pair_len)
    inputs = layer_in.reshape(-1, model_width).astype(jnp.float32)
    normed, attn_norm_back = jax.vjp(layer_norm, inputs, gain_attn, shift_attn)
    normed_low = normed.astype(jnp.bfloat16)
    mixed = jnp.dot(normed_low, qkv_full, preferred_element_type=jnp.float32)
    query = ((mixed[:, :model_width] + bias_query) * 0.125).astype(jnp.bfloat16)
    keys = mixed[:, model_width : 2 * model_width].astype(jnp.bfloat16)
    values = (mixed[:, 2 * model_width :] + bias_value).astype(jnp.bfloat16)

    def to_groups(array):
        return array.reshape(seq_count, 2, half_rows, fsdp_size, group_width)

    def to_pairs(array):
        return array.reshape(seq_count, 2, block_len, 1, group_width)

    query_heads, key_heads, value_heads = (
        lax.all_to_all(to_groups(query), "fsdp", split_axis=3, concat_axis=2, tiled=True),
        lax.all_to_all(to_groups(keys), "fsdp", split_axis=3, concat_axis=2, tiled=True),
        lax.all_to_all(to_groups(values), "fsdp", split_axis=3, concat_axis=2, tiled=True),
    )
    query_heads = query_heads.reshape(seq_count, pair_len, group_width)
    own_keys = key_heads.reshape(seq_count, pair_len, group_width)
    own_values = value_heads.reshape(seq_count, pair_len, group_width)
    key_all, value_all = (
        lax.all_gather(
            own_keys.reshape(seq_count, 1, pair_len, group_width), CTX, axis=1, tiled=True
        ),
        lax.all_gather(
            own_values.reshape(seq_count, 1, pair_len, group_width), CTX, axis=1, tiled=True
        ),
    )
    key_all = key_all.reshape(seq_count, -1, group_width)
    value_all = value_all.reshape(seq_count, -1, group_width)
    attended, summary = lax.map(
        attend_forward, (query_heads, key_all, value_all, query_places, key_places)
    )
    attended_rows = lax.all_to_all(
        for_sending(to_pairs(attended)), "fsdp", split_axis=2, concat_axis=3, tiled=True
    ).reshape(-1, model_width)
    branch = jnp.dot(attended_rows, out_full, preferred_element_type=jnp.float32) + bias_out
    middle = inputs + branch
    normed_mlp, mlp_norm_back = jax.vjp(layer_norm, middle, gain_mlp, shift_mlp)
    mlp_low = normed_mlp.astype(jnp.bfloat16)
    hidden = jnp.dot(mlp_low, fc_full, preferred_element_type=jnp.float32) + bias_fc
    activated, gelu_back = jax.vjp(gelu_tanh, hidden)
    activated_low = activated.astype(jnp.bfloat16)
    result = (
        middle + jnp.dot(activated_low, proj_full, preferred_element_type=jnp.float32) + bias_proj
    )
    layer_out = result.astype(jnp.bfloat16).reshape(layer_in.shape)
    grad_rows = out_grad.reshape(-1, model_width)
    grad_result = grad_rows.astype(jnp.float32)
    proj_grad = contract_first(core_major(activated_low, fsdp_size), grad_rows)
    proj_bias_grad = jnp.sum(grad_result, axis=0)
    grad_activated = contract_last(grad_rows, proj_full)
    grad_hidden = gelu_back(grad_activated)[0].astype(jnp.bfloat16)
    fc_grad = contract_first(core_major(mlp_low, fsdp_size), grad_hidden)
    fc_bias_grad = jnp.sum(grad_hidden.astype(jnp.float32), axis=0)
    grad_middle, mlp_gain_grad, mlp_shift_grad = mlp_norm_back(contract_last(grad_hidden, fc_full))
    grad_middle = grad_middle + grad_result
    grad_branch = grad_middle.astype(jnp.bfloat16)
    out_weight_term = contract_first(core_major(attended_rows, fsdp_size), grad_branch)
    out_bias_grad = jnp.sum(grad_branch.astype(jnp.float32), axis=0)
    grad_attended = contract_last(grad_branch, out_full).astype(jnp.bfloat16)
    grad_heads = lax.all_to_all(
        to_groups(grad_attended), "fsdp", split_axis=3, concat_axis=2, tiled=True
    ).reshape(seq_count, pair_len, group_width)
    grad_query, grad_keys, grad_values = lax.map(
        attend_backward,
        (query_heads, key_all, value_all, grad_heads, summary, query_places, key_places),
    )
    kv_grads = jnp.concatenate([grad_keys, grad_values], axis=2).astype(jnp.bfloat16)
    kv_grads = kv_grads.reshape(seq_count, ctx_size, pair_len, 2 * group_width).transpose(1, 0, 2, 3)
    kv_part = lax.psum_scatter(
        kv_grads.reshape(ctx_size * seq_count * pair_len, 2 * group_width),
        CTX,
        scatter_dimension=0,
        tiled=True,
    ).reshape(seq_count, pair_len, 2 * group_width)
    key_part = kv_part[..., :group_width].astype(jnp.float32)
    value_part = kv_part[..., group_width:].astype(jnp.float32)
    key_grad_low = key_part.astype(jnp.bfloat16)
    value_grad_low = value_part.astype(jnp.bfloat16)
    query_back, key_back, value_back = (
        lax.all_to_all(
            for_sending(to_pairs(grad_query)), "fsdp", split_axis=2, concat_axis=3, tiled=True
        ),
        lax.all_to_all(
            for_sending(to_pairs(key_grad_low)), "fsdp", split_axis=2, concat_axis=3, tiled=True
        ),
        lax.all_to_all(
            for_sending(to_pairs(value_grad_low)), "fsdp", split_axis=2, concat_axis=3, tiled=True
        ),
    )
    grad_mixed = jnp.concatenate(
        [
            query_back.reshape(-1, model_width) * 0.125,
            key_back.reshape(-1, model_width),
            value_back.reshape(-1, model_width),
        ],
        axis=1,
    )
    qkv_grad = contract_first(core_major(normed_low, fsdp_size), grad_mixed)
    mixed_float = grad_mixed.astype(jnp.float32)
    query_bias_grad = jnp.sum(mixed_float[:, :model_width], axis=0)
    value_bias_grad = jnp.sum(mixed_float[:, 2 * model_width :], axis=0)
    grad_inputs, attn_gain_grad, attn_shift_grad = attn_norm_back(
        contract_last(grad_mixed, qkv_full)
    )
    in_grad = (grad_inputs + grad_middle).reshape(layer_in.shape)
    weight_totals = finish_weight_grads(
        tuple(reduce_weight_grad(grad) for grad in (qkv_grad, out_weight_term, fc_grad, proj_grad))
    )
    vector_grads = (
        attn_gain_grad,
        attn_shift_grad,
        query_bias_grad,
        value_bias_grad,
        out_bias_grad,
        mlp_gain_grad,
        mlp_shift_grad,
        fc_bias_grad,
        proj_bias_grad,
    )
    packed = jnp.concatenate(
        [grad.astype(jnp.bfloat16).reshape(fsdp_size, -1) for grad in vector_grads], axis=1
    )
    packed = lax.psum_scatter(packed, "fsdp", scatter_dimension=0, tiled=True).reshape(-1)
    packed = lax.psum_scatter(packed, CTX, scatter_dimension=0, tiled=True)
    packed = lax.all_gather(packed, CTX, axis=0, tiled=True).astype(jnp.float32)
    vector_totals = []
    offset = 0
    for grad in vector_grads:
        width = grad.shape[0] // fsdp_size
        vector_totals.append(packed[offset : offset + width])
        offset += width
    totals = weight_totals + tuple(vector_totals)
    return (
        layer_out,
        in_grad,
        totals[4],
        totals[5],
        totals[0],
        totals[6],
        totals[7],
        totals[1],
        totals[8],
        totals[9],
        totals[10],
        totals[2],
        totals[11],
        totals[3],
        totals[12],
    )


def solution(mesh):
    ctx_count, fsdp_count = mesh.devices.shape
    mesh = jax.sharding.Mesh(
        mesh.devices.reshape(ctx_count // 2, 2, fsdp_count), ("zc", "core", "fsdp")
    )
    placed = (
        P(None, CTX, None, "fsdp", None),
        P(None, CTX, None, "fsdp", None),
        P(),
        P("fsdp"),
        P("fsdp"),
        P("fsdp", None),
        P("fsdp"),
        P("fsdp"),
        P("fsdp", None),
        P("fsdp"),
        P("fsdp"),
        P("fsdp"),
        P("fsdp", None),
        P("fsdp"),
        P("fsdp", None),
        P("fsdp"),
    )
    return jax.shard_map(
        shards,
        mesh=mesh,
        in_specs=placed,
        out_specs=(
            P(None, CTX, None, "fsdp", None),
            P(None, CTX, None, "fsdp", None),
            P("fsdp"),
            P("fsdp"),
            P("fsdp", None),
            P("fsdp"),
            P("fsdp"),
            P("fsdp", None),
            P("fsdp"),
            P("fsdp"),
            P("fsdp"),
            P("fsdp", None),
            P("fsdp"),
            P("fsdp", None),
            P("fsdp"),
        ),
        check_vma=False,
    )
```

```python
import jax
import jax.numpy as jnp
from jax import lax
from jax.sharding import PartitionSpec as P

HD = 64


norm_eps = 1e-05
masked_score = -1e30


def for_sending(array):
    return jax.tree.map(lambda a: a.astype(jnp.bfloat16) if a.dtype == jnp.float32 else a, array)


def layer_norm(values, gain, shift):
    average = jnp.mean(values, axis=-1, keepdims=True)
    centred = values - average
    spread = jnp.mean(centred * centred, axis=-1, keepdims=True)
    return centred * lax.rsqrt(spread + norm_eps) * gain + shift


def gelu_tanh(values):
    return jax.nn.gelu(values, approximate=True)


def contract_last(left, right):
    return lax.dot_general(
        left, right, (((1,), (1,)), ((), ())), preferred_element_type=jnp.float32
    )


def contract_first(left, right):
    return lax.dot_general(
        left, right, (((0,), (0,)), ((), ())), preferred_element_type=jnp.float32
    )


def head_scores(query, keys, query_places, key_places):
    scores = contract_last(query, keys)
    return jnp.where(key_places[None, :] <= query_places[:, None], scores, masked_score)


def score_grads(query, keys, values, grad_out, summary, row_sum, query_places, key_places):
    scores = head_scores(query, keys, query_places, key_places)
    probs = jnp.exp(scores - summary[:, None])
    grad_probs = contract_last(grad_out, values)
    row_sum = jnp.sum(probs * grad_probs, axis=1)
    grad_scores = (probs * (grad_probs - row_sum[:, None])).astype(jnp.bfloat16)
    return (probs.astype(jnp.bfloat16), grad_scores, row_sum)


def attend_forward(items):
    query, keys, values, query_places, key_places = items
    outputs = []
    summaries = []
    for head_index in range(query.shape[1] // HD):
        columns = slice(head_index * HD, (head_index + 1) * HD)
        scores = head_scores(query[:, columns], keys[:, columns], query_places, key_places)
        row_peak = jnp.max(scores, axis=1, keepdims=True)
        raised = jnp.exp(scores - row_peak)
        row_total = jnp.sum(raised, axis=1, keepdims=True)
        weights = (raised / row_total).astype(jnp.bfloat16)
        outputs.append(
            jnp.dot(weights, values[:, columns], preferred_element_type=jnp.float32).astype(
                jnp.bfloat16
            )
        )
        summaries.append(row_peak[:, 0] + jnp.log(row_total[:, 0]))
    return (jnp.concatenate(outputs, axis=1), jnp.stack(summaries, axis=1))


def attend_backward(items):
    query, keys, values, grad_out, summary, query_places, key_places = items
    query_parts, key_parts, value_parts = ([], [], [])
    for head_index in range(query.shape[1] // HD):
        columns = slice(head_index * HD, (head_index + 1) * HD)
        probs_low, grad_scores, row_sum = score_grads(
            query[:, columns],
            keys[:, columns],
            values[:, columns],
            grad_out[:, columns],
            summary[:, head_index],
            None,
            query_places,
            key_places,
        )
        query_parts.append(
            jnp.dot(grad_scores, keys[:, columns], preferred_element_type=jnp.float32).astype(
                jnp.bfloat16
            )
        )
        key_parts.append(contract_first(grad_scores, query[:, columns]))
        value_parts.append(contract_first(probs_low, grad_out[:, columns]))
    return (
        jnp.concatenate(query_parts, axis=1),
        jnp.concatenate(key_parts, axis=1),
        jnp.concatenate(value_parts, axis=1),
    )


CTX = ("zc", "core")


def gather_weight(shard):
    half = shard.shape[0] // 2
    piece = lax.dynamic_slice_in_dim(shard, lax.axis_index("core") * half, half, 0)
    fsdp_size = lax.axis_size("fsdp")
    pieces = lax.all_to_all(
        jnp.broadcast_to(piece[None], (fsdp_size,) + piece.shape),
        "fsdp",
        split_axis=0,
        concat_axis=0,
        tiled=True,
    )
    whole = lax.all_gather(pieces, "core", axis=1, tiled=True)
    return whole.reshape(-1, shard.shape[1])


def core_major(rows, fsdp_size):
    count, width = rows.shape
    return rows.reshape(count, fsdp_size, 2, width // (2 * fsdp_size)).transpose(0, 2, 1, 3).reshape(
        count, width
    )


def reduce_weight_grad(grad):
    grad = lax.psum_scatter(grad.astype(jnp.bfloat16), "core", scatter_dimension=0, tiled=True)
    fsdp_size = lax.axis_size("fsdp")
    blocks = lax.all_to_all(
        grad.reshape((fsdp_size, -1) + grad.shape[1:]), "fsdp", split_axis=0, concat_axis=0, tiled=True
    )
    grad = jnp.sum(blocks.astype(jnp.float32), axis=0).astype(jnp.bfloat16)
    grad = lax.psum_scatter(grad, "zc", scatter_dimension=0, tiled=True)
    grad = lax.all_gather(grad, "zc", axis=0, tiled=True)
    grad = lax.all_gather(grad, "core", axis=0, tiled=True)
    return grad.astype(jnp.float32)


def shards(
    layer_in,
    out_grad,
    block_pairs,
    attn_gain,
    attn_shift,
    qkv_weight,
    query_bias,
    value_bias,
    out_weight,
    out_bias,
    mlp_gain,
    mlp_shift,
    fc_weight,
    fc_bias,
    proj_weight,
    proj_bias,
):
    fsdp_size = lax.axis_size("fsdp")
    ctx_size = lax.axis_size("zc") * lax.axis_size("core")
    seq_count = layer_in.shape[0]
    half_rows = layer_in.shape[3]
    model_width = layer_in.shape[4]
    block_len = half_rows * fsdp_size
    pair_len = 2 * block_len
    group_width = model_width // fsdp_size
    gathered = (
        gather_weight(qkv_weight),
        gather_weight(out_weight),
        gather_weight(fc_weight),
        gather_weight(proj_weight),
    )
    qkv_full, out_full, fc_full, proj_full = (gathered[0], gathered[1], gathered[2], gathered[3])
    vector_shards = (
        attn_gain,
        attn_shift,
        query_bias,
        value_bias,
        out_bias,
        mlp_gain,
        mlp_shift,
        fc_bias,
        proj_bias,
    )
    vector_pieces = lax.all_gather(jnp.concatenate(vector_shards), "fsdp", axis=0, tiled=False)
    vectors = []
    start = 0
    for shard in vector_shards:
        vectors.append(vector_pieces[:, start : start + shard.shape[0]].reshape(-1).astype(jnp.float32))
        start += shard.shape[0]
    (
        gain_attn,
        shift_attn,
        bias_query,
        bias_value,
        bias_out,
        gain_mlp,
        shift_mlp,
        bias_fc,
        bias_proj,
    ) = vectors
    halves = jnp.stack([block_pairs, 2 * ctx_size - 1 - block_pairs], axis=2)
    key_places = (halves[..., None] * block_len + jnp.arange(block_len, dtype=jnp.int32)).reshape(
        seq_count, ctx_size, pair_len
    )
    query_places = lax.dynamic_slice_in_dim(key_places, lax.axis_index(CTX), 1, 1).reshape(
        seq_count, pair_len
    )
    key_places = key_places.reshape(seq_count, ctx_size * pair_len)
    inputs = layer_in.reshape(-1, model_width).astype(jnp.float32)
    normed, attn_norm_back = jax.vjp(layer_norm, inputs, gain_attn, shift_attn)
    normed_low = normed.astype(jnp.bfloat16)
    mixed = jnp.dot(normed_low, qkv_full, preferred_element_type=jnp.float32)
    query = ((mixed[:, :model_width] + bias_query) * 0.125).astype(jnp.bfloat16)
    keys = mixed[:, model_width : 2 * model_width].astype(jnp.bfloat16)
    values = (mixed[:, 2 * model_width :] + bias_value).astype(jnp.bfloat16)

    def to_groups(array):
        return array.reshape(seq_count, 2, half_rows, fsdp_size, group_width)

    def to_pairs(array):
        return array.reshape(seq_count, 2, block_len, 1, group_width)

    query_heads, key_heads, value_heads = (
        lax.all_to_all(to_groups(query), "fsdp", split_axis=3, concat_axis=2, tiled=True),
        lax.all_to_all(to_groups(keys), "fsdp", split_axis=3, concat_axis=2, tiled=True),
        lax.all_to_all(to_groups(values), "fsdp", split_axis=3, concat_axis=2, tiled=True),
    )
    query_heads = query_heads.reshape(seq_count, pair_len, group_width)
    own_keys = key_heads.reshape(seq_count, pair_len, group_width)
    own_values = value_heads.reshape(seq_count, pair_len, group_width)
    key_all, value_all = (
        lax.all_gather(
            own_keys.reshape(seq_count, 1, pair_len, group_width), CTX, axis=1, tiled=True
        ),
        lax.all_gather(
            own_values.reshape(seq_count, 1, pair_len, group_width), CTX, axis=1, tiled=True
        ),
    )
    key_all = key_all.reshape(seq_count, -1, group_width)
    value_all = value_all.reshape(seq_count, -1, group_width)
    attended, summary = lax.map(
        attend_forward, (query_heads, key_all, value_all, query_places, key_places)
    )
    attended_rows = lax.all_to_all(
        for_sending(to_pairs(attended)), "fsdp", split_axis=2, concat_axis=3, tiled=True
    ).reshape(-1, model_width)
    branch = jnp.dot(attended_rows, out_full, preferred_element_type=jnp.float32) + bias_out
    middle = inputs + branch
    normed_mlp, mlp_norm_back = jax.vjp(layer_norm, middle, gain_mlp, shift_mlp)
    mlp_low = normed_mlp.astype(jnp.bfloat16)
    hidden = jnp.dot(mlp_low, fc_full, preferred_element_type=jnp.float32) + bias_fc
    activated, gelu_back = jax.vjp(gelu_tanh, hidden)
    activated_low = activated.astype(jnp.bfloat16)
    result = (
        middle + jnp.dot(activated_low, proj_full, preferred_element_type=jnp.float32) + bias_proj
    )
    layer_out = result.astype(jnp.bfloat16).reshape(layer_in.shape)
    grad_rows = out_grad.reshape(-1, model_width)
    grad_result = grad_rows.astype(jnp.float32)
    proj_grad = contract_first(core_major(activated_low, fsdp_size), grad_rows)
    proj_bias_grad = jnp.sum(grad_result, axis=0)
    grad_activated = contract_last(grad_rows, proj_full)
    grad_hidden = gelu_back(grad_activated)[0].astype(jnp.bfloat16)
    fc_grad = contract_first(core_major(mlp_low, fsdp_size), grad_hidden)
    fc_bias_grad = jnp.sum(grad_hidden.astype(jnp.float32), axis=0)
    grad_middle, mlp_gain_grad, mlp_shift_grad = mlp_norm_back(contract_last(grad_hidden, fc_full))
    grad_middle = grad_middle + grad_result
    grad_branch = grad_middle.astype(jnp.bfloat16)
    out_weight_term = contract_first(core_major(attended_rows, fsdp_size), grad_branch)
    out_bias_grad = jnp.sum(grad_branch.astype(jnp.float32), axis=0)
    grad_attended = contract_last(grad_branch, out_full).astype(jnp.bfloat16)
    grad_heads = lax.all_to_all(
        to_groups(grad_attended), "fsdp", split_axis=3, concat_axis=2, tiled=True
    ).reshape(seq_count, pair_len, group_width)
    grad_query, grad_keys, grad_values = lax.map(
        attend_backward,
        (query_heads, key_all, value_all, grad_heads, summary, query_places, key_places),
    )
    kv_grads = jnp.concatenate([grad_keys, grad_values], axis=2).astype(jnp.bfloat16)
    kv_grads = kv_grads.reshape(seq_count, ctx_size, pair_len, 2 * group_width).transpose(1, 0, 2, 3)
    kv_part = lax.psum_scatter(
        kv_grads.reshape(ctx_size * seq_count * pair_len, 2 * group_width),
        CTX,
        scatter_dimension=0,
        tiled=True,
    ).reshape(seq_count, pair_len, 2 * group_width)
    key_part = kv_part[..., :group_width].astype(jnp.float32)
    value_part = kv_part[..., group_width:].astype(jnp.float32)
    key_grad_low = key_part.astype(jnp.bfloat16)
    value_grad_low = value_part.astype(jnp.bfloat16)
    query_back, key_back, value_back = (
        lax.all_to_all(
            for_sending(to_pairs(grad_query)), "fsdp", split_axis=2, concat_axis=3, tiled=True
        ),
        lax.all_to_all(
            for_sending(to_pairs(key_grad_low)), "fsdp", split_axis=2, concat_axis=3, tiled=True
        ),
        lax.all_to_all(
            for_sending(to_pairs(value_grad_low)), "fsdp", split_axis=2, concat_axis=3, tiled=True
        ),
    )
    grad_mixed = jnp.concatenate(
        [
            query_back.reshape(-1, model_width) * 0.125,
            key_back.reshape(-1, model_width),
            value_back.reshape(-1, model_width),
        ],
        axis=1,
    )
    qkv_grad = contract_first(core_major(normed_low, fsdp_size), grad_mixed)
    mixed_float = grad_mixed.astype(jnp.float32)
    query_bias_grad = jnp.sum(mixed_float[:, :model_width], axis=0)
    value_bias_grad = jnp.sum(mixed_float[:, 2 * model_width :], axis=0)
    grad_inputs, attn_gain_grad, attn_shift_grad = attn_norm_back(
        contract_last(grad_mixed, qkv_full)
    )
    in_grad = (grad_inputs + grad_middle).reshape(layer_in.shape)
    weight_totals = tuple(
        reduce_weight_grad(grad) for grad in (qkv_grad, out_weight_term, fc_grad, proj_grad)
    )
    vector_grads = (
        attn_gain_grad,
        attn_shift_grad,
        query_bias_grad,
        value_bias_grad,
        out_bias_grad,
        mlp_gain_grad,
        mlp_shift_grad,
        fc_bias_grad,
        proj_bias_grad,
    )
    packed = jnp.concatenate(
        [grad.astype(jnp.bfloat16).reshape(fsdp_size, -1) for grad in vector_grads], axis=1
    )
    packed = lax.psum_scatter(packed, "fsdp", scatter_dimension=0, tiled=True).reshape(-1)
    packed = lax.psum_scatter(packed, CTX, scatter_dimension=0, tiled=True)
    packed = lax.all_gather(packed, CTX, axis=0, tiled=True).astype(jnp.float32)
    vector_totals = []
    offset = 0
    for grad in vector_grads:
        width = grad.shape[0] // fsdp_size
        vector_totals.append(packed[offset : offset + width])
        offset += width
    totals = weight_totals + tuple(vector_totals)
    return (
        layer_out,
        in_grad,
        totals[4],
        totals[5],
        totals[0],
        totals[6],
        totals[7],
        totals[1],
        totals[8],
        totals[9],
        totals[10],
        totals[2],
        totals[11],
        totals[3],
        totals[12],
    )


def solution(mesh):
    ctx_count, fsdp_count = mesh.devices.shape
    mesh = jax.sharding.Mesh(
        mesh.devices.reshape(ctx_count // 2, 2, fsdp_count), ("zc", "core", "fsdp")
    )
    placed = (
        P(None, CTX, None, "fsdp", None),
        P(None, CTX, None, "fsdp", None),
        P(),
        P("fsdp"),
        P("fsdp"),
        P("fsdp", None),
        P("fsdp"),
        P("fsdp"),
        P("fsdp", None),
        P("fsdp"),
        P("fsdp"),
        P("fsdp"),
        P("fsdp", None),
        P("fsdp"),
        P("fsdp", None),
        P("fsdp"),
    )
    return jax.shard_map(
        shards,
        mesh=mesh,
        in_specs=placed,
        out_specs=(
            P(None, CTX, None, "fsdp", None),
            P(None, CTX, None, "fsdp", None),
            P("fsdp"),
            P("fsdp"),
            P("fsdp", None),
            P("fsdp"),
            P("fsdp"),
            P("fsdp", None),
            P("fsdp"),
            P("fsdp"),
            P("fsdp"),
            P("fsdp", None),
            P("fsdp"),
            P("fsdp", None),
            P("fsdp"),
        ),
        check_vma=False,
    )
```

```python
import jax
import jax.numpy as jnp
from jax import lax
from jax.sharding import PartitionSpec as P

HD = 64


norm_eps = 1e-05
masked_score = -1e30


def for_sending(array):
    return jax.tree.map(lambda a: a.astype(jnp.bfloat16) if a.dtype == jnp.float32 else a, array)


def layer_norm(values, gain, shift):
    average = jnp.mean(values, axis=-1, keepdims=True)
    centred = values - average
    spread = jnp.mean(centred * centred, axis=-1, keepdims=True)
    return centred * lax.rsqrt(spread + norm_eps) * gain + shift


def gelu_tanh(values):
    return jax.nn.gelu(values, approximate=True)


def contract_last(left, right):
    return lax.dot_general(
        left, right, (((1,), (1,)), ((), ())), preferred_element_type=jnp.float32
    )


def contract_first(left, right):
    return lax.dot_general(
        left, right, (((0,), (0,)), ((), ())), preferred_element_type=jnp.float32
    )


def head_scores(query, keys, query_places, key_places):
    scores = contract_last(query, keys)
    return jnp.where(key_places[None, :] <= query_places[:, None], scores, masked_score)


def score_grads(query, keys, values, grad_out, summary, row_sum, query_places, key_places):
    scores = head_scores(query, keys, query_places, key_places)
    probs = jnp.exp(scores - summary[:, None])
    grad_probs = contract_last(grad_out, values)
    row_sum = jnp.sum(probs * grad_probs, axis=1)
    grad_scores = (probs * (grad_probs - row_sum[:, None])).astype(jnp.bfloat16)
    return (probs.astype(jnp.bfloat16), grad_scores, row_sum)


def attend_forward(items):
    query, keys, values, query_places, key_places = items
    outputs = []
    summaries = []
    for head_index in range(query.shape[1] // HD):
        columns = slice(head_index * HD, (head_index + 1) * HD)
        scores = head_scores(query[:, columns], keys[:, columns], query_places, key_places)
        row_peak = jnp.max(scores, axis=1, keepdims=True)
        raised = jnp.exp(scores - row_peak)
        row_total = jnp.sum(raised, axis=1, keepdims=True)
        weights = (raised / row_total).astype(jnp.bfloat16)
        outputs.append(
            jnp.dot(weights, values[:, columns], preferred_element_type=jnp.float32).astype(
                jnp.bfloat16
            )
        )
        summaries.append(row_peak[:, 0] + jnp.log(row_total[:, 0]))
    return (jnp.concatenate(outputs, axis=1), jnp.stack(summaries, axis=1))


def attend_backward(items):
    query, keys, values, grad_out, summary, query_places, key_places = items
    query_parts, key_parts, value_parts = ([], [], [])
    for head_index in range(query.shape[1] // HD):
        columns = slice(head_index * HD, (head_index + 1) * HD)
        probs_low, grad_scores, row_sum = score_grads(
            query[:, columns],
            keys[:, columns],
            values[:, columns],
            grad_out[:, columns],
            summary[:, head_index],
            None,
            query_places,
            key_places,
        )
        query_parts.append(
            jnp.dot(grad_scores, keys[:, columns], preferred_element_type=jnp.float32).astype(
                jnp.bfloat16
            )
        )
        key_parts.append(contract_first(grad_scores, query[:, columns]))
        value_parts.append(contract_first(probs_low, grad_out[:, columns]))
    return (
        jnp.concatenate(query_parts, axis=1),
        jnp.concatenate(key_parts, axis=1),
        jnp.concatenate(value_parts, axis=1),
    )


CTX = ("zc", "core")


def gather_weight(shard):
    half = shard.shape[0] // 2
    piece = lax.dynamic_slice_in_dim(shard, lax.axis_index("core") * half, half, 0)
    fsdp_size = lax.axis_size("fsdp")
    pieces = lax.all_to_all(
        jnp.broadcast_to(piece[None], (fsdp_size,) + piece.shape),
        "fsdp",
        split_axis=0,
        concat_axis=0,
        tiled=True,
    )
    whole = lax.all_gather(pieces, "core", axis=1, tiled=True)
    return whole.reshape(-1, shard.shape[1])


def core_major(rows, fsdp_size):
    count, width = rows.shape
    return rows.reshape(count, fsdp_size, 2, width // (2 * fsdp_size)).transpose(0, 2, 1, 3).reshape(
        count, width
    )


def reduce_weight_grad(grad):
    grad = lax.psum_scatter(grad.astype(jnp.bfloat16), "core", scatter_dimension=0, tiled=True)
    fsdp_size = lax.axis_size("fsdp")
    blocks = lax.all_to_all(
        grad.reshape((fsdp_size, -1) + grad.shape[1:]), "fsdp", split_axis=0, concat_axis=0, tiled=True
    )
    grad = jnp.sum(blocks.astype(jnp.float32), axis=0).astype(jnp.bfloat16)
    grad = lax.psum_scatter(grad, "zc", scatter_dimension=0, tiled=True)
    grad = lax.all_gather(grad, "zc", axis=0, tiled=True)
    grad = lax.all_gather(grad, "core", axis=0, tiled=True)
    return grad.astype(jnp.float32)


def shards(
    layer_in,
    out_grad,
    block_pairs,
    attn_gain,
    attn_shift,
    qkv_weight,
    query_bias,
    value_bias,
    out_weight,
    out_bias,
    mlp_gain,
    mlp_shift,
    fc_weight,
    fc_bias,
    proj_weight,
    proj_bias,
):
    fsdp_size = lax.axis_size("fsdp")
    ctx_size = lax.axis_size("zc") * lax.axis_size("core")
    seq_count = layer_in.shape[0]
    half_rows = layer_in.shape[3]
    model_width = layer_in.shape[4]
    block_len = half_rows * fsdp_size
    pair_len = 2 * block_len
    group_width = model_width // fsdp_size
    gathered = (
        gather_weight(qkv_weight),
        gather_weight(out_weight),
        gather_weight(fc_weight),
        gather_weight(proj_weight),
    )
    qkv_full, out_full, fc_full, proj_full = (gathered[0], gathered[1], gathered[2], gathered[3])
    vector_shards = (
        attn_gain,
        attn_shift,
        query_bias,
        value_bias,
        out_bias,
        mlp_gain,
        mlp_shift,
        fc_bias,
        proj_bias,
    )
    vector_pieces = lax.all_gather(jnp.concatenate(vector_shards), "fsdp", axis=0, tiled=False)
    vectors = []
    start = 0
    for shard in vector_shards:
        vectors.append(vector_pieces[:, start : start + shard.shape[0]].reshape(-1).astype(jnp.float32))
        start += shard.shape[0]
    (
        gain_attn,
        shift_attn,
        bias_query,
        bias_value,
        bias_out,
        gain_mlp,
        shift_mlp,
        bias_fc,
        bias_proj,
    ) = vectors
    halves = jnp.stack([block_pairs, 2 * ctx_size - 1 - block_pairs], axis=2)
    key_places = (halves[..., None] * block_len + jnp.arange(block_len, dtype=jnp.int32)).reshape(
        seq_count, ctx_size, pair_len
    )
    query_places = lax.dynamic_slice_in_dim(key_places, lax.axis_index(CTX), 1, 1).reshape(
        seq_count, pair_len
    )
    key_places = key_places.reshape(seq_count, ctx_size * pair_len)
    inputs = layer_in.reshape(-1, model_width).astype(jnp.float32)
    normed, attn_norm_back = jax.vjp(layer_norm, inputs, gain_attn, shift_attn)
    normed_low = normed.astype(jnp.bfloat16)
    mixed = jnp.dot(normed_low, qkv_full, preferred_element_type=jnp.float32)
    query = ((mixed[:, :model_width] + bias_query) * 0.125).astype(jnp.bfloat16)
    keys = mixed[:, model_width : 2 * model_width].astype(jnp.bfloat16)
    values = (mixed[:, 2 * model_width :] + bias_value).astype(jnp.bfloat16)

    def to_groups(array):
        return array.reshape(seq_count, 2, half_rows, fsdp_size, group_width)

    def to_pairs(array):
        return array.reshape(seq_count, 2, block_len, 1, group_width)

    query_heads, key_heads, value_heads = (
        lax.all_to_all(to_groups(query), "fsdp", split_axis=3, concat_axis=2, tiled=True),
        lax.all_to_all(to_groups(keys), "fsdp", split_axis=3, concat_axis=2, tiled=True),
        lax.all_to_all(to_groups(values), "fsdp", split_axis=3, concat_axis=2, tiled=True),
    )
    query_heads = query_heads.reshape(seq_count, pair_len, group_width)
    own_keys = key_heads.reshape(seq_count, pair_len, group_width)
    own_values = value_heads.reshape(seq_count, pair_len, group_width)
    key_all, value_all = (
        lax.all_gather(
            own_keys.reshape(seq_count, 1, pair_len, group_width), CTX, axis=1, tiled=True
        ),
        lax.all_gather(
            own_values.reshape(seq_count, 1, pair_len, group_width), CTX, axis=1, tiled=True
        ),
    )
    key_all = key_all.reshape(seq_count, -1, group_width)
    value_all = value_all.reshape(seq_count, -1, group_width)
    attended, summary = lax.map(
        attend_forward, (query_heads, key_all, value_all, query_places, key_places)
    )
    attended_rows = lax.all_to_all(
        for_sending(to_pairs(attended)), "fsdp", split_axis=2, concat_axis=3, tiled=True
    ).reshape(-1, model_width)
    branch = jnp.dot(attended_rows, out_full, preferred_element_type=jnp.float32) + bias_out
    middle = inputs + branch
    normed_mlp, mlp_norm_back = jax.vjp(layer_norm, middle, gain_mlp, shift_mlp)
    mlp_low = normed_mlp.astype(jnp.bfloat16)
    hidden = jnp.dot(mlp_low, fc_full, preferred_element_type=jnp.float32) + bias_fc
    activated, gelu_back = jax.vjp(gelu_tanh, hidden)
    activated_low = activated.astype(jnp.bfloat16)
    result = (
        middle + jnp.dot(activated_low, proj_full, preferred_element_type=jnp.float32) + bias_proj
    )
    layer_out = result.astype(jnp.bfloat16).reshape(layer_in.shape)
    grad_rows = out_grad.reshape(-1, model_width)
    grad_result = grad_rows.astype(jnp.float32)
    proj_grad = contract_first(core_major(activated_low, fsdp_size), grad_rows)
    proj_bias_grad = jnp.sum(grad_result, axis=0)
    grad_activated = contract_last(grad_rows, proj_full)
    grad_hidden = gelu_back(grad_activated)[0].astype(jnp.bfloat16)
    fc_grad = contract_first(core_major(mlp_low, fsdp_size), grad_hidden)
    fc_bias_grad = jnp.sum(grad_hidden.astype(jnp.float32), axis=0)
    grad_middle, mlp_gain_grad, mlp_shift_grad = mlp_norm_back(contract_last(grad_hidden, fc_full))
    grad_middle = grad_middle + grad_result
    grad_branch = grad_middle.astype(jnp.bfloat16)
    out_weight_term = contract_first(core_major(attended_rows, fsdp_size), grad_branch)
    out_bias_grad = jnp.sum(grad_branch.astype(jnp.float32), axis=0)
    grad_attended = contract_last(grad_branch, out_full).astype(jnp.bfloat16)
    grad_heads = lax.all_to_all(
        to_groups(grad_attended), "fsdp", split_axis=3, concat_axis=2, tiled=True
    ).reshape(seq_count, pair_len, group_width)
    grad_query, grad_keys, grad_values = lax.map(
        attend_backward,
        (query_heads, key_all, value_all, grad_heads, summary, query_places, key_places),
    )
    kv_grads = jnp.concatenate([grad_keys, grad_values], axis=2).astype(jnp.bfloat16)
    kv_grads = kv_grads.reshape(seq_count, ctx_size, pair_len, 2 * group_width).transpose(1, 0, 2, 3)
    kv_part = lax.psum_scatter(
        kv_grads.reshape(ctx_size * seq_count * pair_len, 2 * group_width),
        CTX,
        scatter_dimension=0,
        tiled=True,
    ).reshape(seq_count, pair_len, 2 * group_width)
    key_part = kv_part[..., :group_width].astype(jnp.float32)
    value_part = kv_part[..., group_width:].astype(jnp.float32)
    key_grad_low = key_part.astype(jnp.bfloat16)
    value_grad_low = value_part.astype(jnp.bfloat16)
    query_back, key_back, value_back = (
        lax.all_to_all(
            for_sending(to_pairs(grad_query)), "fsdp", split_axis=2, concat_axis=3, tiled=True
        ),
        lax.all_to_all(
            for_sending(to_pairs(key_grad_low)), "fsdp", split_axis=2, concat_axis=3, tiled=True
        ),
        lax.all_to_all(
            for_sending(to_pairs(value_grad_low)), "fsdp", split_axis=2, concat_axis=3, tiled=True
        ),
    )
    grad_mixed = jnp.concatenate(
        [
            query_back.reshape(-1, model_width) * 0.125,
            key_back.reshape(-1, model_width),
            value_back.reshape(-1, model_width),
        ],
        axis=1,
    )
    qkv_grad = contract_first(core_major(normed_low, fsdp_size), grad_mixed)
    mixed_float = grad_mixed.astype(jnp.float32)
    query_bias_grad = jnp.sum(mixed_float[:, :model_width], axis=0)
    value_bias_grad = jnp.sum(mixed_float[:, 2 * model_width :], axis=0)
    grad_inputs, attn_gain_grad, attn_shift_grad = attn_norm_back(
        contract_last(grad_mixed, qkv_full)
    )
    in_grad = (grad_inputs + grad_middle).reshape(layer_in.shape)
    weight_totals = tuple(
        reduce_weight_grad(grad) for grad in (qkv_grad, out_weight_term, fc_grad, proj_grad)
    )
    vector_grads = (
        attn_gain_grad,
        attn_shift_grad,
        query_bias_grad,
        value_bias_grad,
        out_bias_grad,
        mlp_gain_grad,
        mlp_shift_grad,
        fc_bias_grad,
        proj_bias_grad,
    )
    packed = jnp.concatenate([grad.reshape(fsdp_size, -1) for grad in vector_grads], axis=1)
    packed = lax.psum(packed.astype(jnp.float32), CTX + ("fsdp",))
    packed = lax.dynamic_index_in_dim(packed, lax.axis_index("fsdp"), 0, keepdims=False)
    vector_totals = []
    offset = 0
    for grad in vector_grads:
        width = grad.shape[0] // fsdp_size
        vector_totals.append(packed[offset : offset + width])
        offset += width
    totals = weight_totals + tuple(vector_totals)
    return (
        layer_out,
        in_grad,
        totals[4],
        totals[5],
        totals[0],
        totals[6],
        totals[7],
        totals[1],
        totals[8],
        totals[9],
        totals[10],
        totals[2],
        totals[11],
        totals[3],
        totals[12],
    )


def solution(mesh):
    ctx_count, fsdp_count = mesh.devices.shape
    mesh = jax.sharding.Mesh(
        mesh.devices.reshape(ctx_count // 2, 2, fsdp_count), ("zc", "core", "fsdp")
    )
    placed = (
        P(None, CTX, None, "fsdp", None),
        P(None, CTX, None, "fsdp", None),
        P(),
        P("fsdp"),
        P("fsdp"),
        P("fsdp", None),
        P("fsdp"),
        P("fsdp"),
        P("fsdp", None),
        P("fsdp"),
        P("fsdp"),
        P("fsdp"),
        P("fsdp", None),
        P("fsdp"),
        P("fsdp", None),
        P("fsdp"),
    )
    return jax.shard_map(
        shards,
        mesh=mesh,
        in_specs=placed,
        out_specs=(
            P(None, CTX, None, "fsdp", None),
            P(None, CTX, None, "fsdp", None),
            P("fsdp"),
            P("fsdp"),
            P("fsdp", None),
            P("fsdp"),
            P("fsdp"),
            P("fsdp", None),
            P("fsdp"),
            P("fsdp"),
            P("fsdp"),
            P("fsdp", None),
            P("fsdp"),
            P("fsdp", None),
            P("fsdp"),
        ),
        check_vma=False,
    )
```

```python
import jax
import jax.numpy as jnp
from jax import lax
from jax.sharding import PartitionSpec as P

HD = 64


norm_eps = 1e-05
masked_score = -1e30


def for_sending(array):
    return jax.tree.map(lambda a: a.astype(jnp.bfloat16) if a.dtype == jnp.float32 else a, array)


def layer_norm(values, gain, shift):
    average = jnp.mean(values, axis=-1, keepdims=True)
    centred = values - average
    spread = jnp.mean(centred * centred, axis=-1, keepdims=True)
    return centred * lax.rsqrt(spread + norm_eps) * gain + shift


def gelu_tanh(values):
    return jax.nn.gelu(values, approximate=True)


def contract_last(left, right):
    return lax.dot_general(
        left, right, (((1,), (1,)), ((), ())), preferred_element_type=jnp.float32
    )


def contract_first(left, right):
    return lax.dot_general(
        left, right, (((0,), (0,)), ((), ())), preferred_element_type=jnp.float32
    )


def head_scores(query, keys, query_places, key_places):
    scores = contract_last(query, keys)
    return jnp.where(key_places[None, :] <= query_places[:, None], scores, masked_score)


def score_grads(query, keys, values, grad_out, summary, row_sum, query_places, key_places):
    scores = head_scores(query, keys, query_places, key_places)
    probs = jnp.exp(scores - summary[:, None])
    grad_probs = contract_last(grad_out, values)
    row_sum = jnp.sum(probs * grad_probs, axis=1)
    grad_scores = (probs * (grad_probs - row_sum[:, None])).astype(jnp.bfloat16)
    return (probs.astype(jnp.bfloat16), grad_scores, row_sum)


def attend_forward(items):
    query, keys, values, query_places, key_places = items
    outputs = []
    summaries = []
    for head_index in range(query.shape[1] // HD):
        columns = slice(head_index * HD, (head_index + 1) * HD)
        scores = head_scores(query[:, columns], keys[:, columns], query_places, key_places)
        row_peak = jnp.max(scores, axis=1, keepdims=True)
        raised = jnp.exp(scores - row_peak)
        row_total = jnp.sum(raised, axis=1, keepdims=True)
        weights = (raised / row_total).astype(jnp.bfloat16)
        outputs.append(
            jnp.dot(weights, values[:, columns], preferred_element_type=jnp.float32).astype(
                jnp.bfloat16
            )
        )
        summaries.append(row_peak[:, 0] + jnp.log(row_total[:, 0]))
    return (jnp.concatenate(outputs, axis=1), jnp.stack(summaries, axis=1))


def attend_backward(items):
    query, keys, values, grad_out, summary, query_places, key_places = items
    query_parts, key_parts, value_parts = ([], [], [])
    for head_index in range(query.shape[1] // HD):
        columns = slice(head_index * HD, (head_index + 1) * HD)
        probs_low, grad_scores, row_sum = score_grads(
            query[:, columns],
            keys[:, columns],
            values[:, columns],
            grad_out[:, columns],
            summary[:, head_index],
            None,
            query_places,
            key_places,
        )
        query_parts.append(
            jnp.dot(grad_scores, keys[:, columns], preferred_element_type=jnp.float32).astype(
                jnp.bfloat16
            )
        )
        key_parts.append(contract_first(grad_scores, query[:, columns]))
        value_parts.append(contract_first(probs_low, grad_out[:, columns]))
    return (
        jnp.concatenate(query_parts, axis=1),
        jnp.concatenate(key_parts, axis=1),
        jnp.concatenate(value_parts, axis=1),
    )


CTX = ("zc", "core")


def gather_weight(shard):
    half = shard.shape[0] // 2
    piece = lax.dynamic_slice_in_dim(shard, lax.axis_index("core") * half, half, 0)
    fsdp_size = lax.axis_size("fsdp")
    pieces = lax.all_to_all(
        jnp.broadcast_to(piece[None], (fsdp_size,) + piece.shape),
        "fsdp",
        split_axis=0,
        concat_axis=0,
        tiled=True,
    )
    whole = lax.all_gather(pieces, "core", axis=1, tiled=True)
    return whole.reshape(-1, shard.shape[1])


def core_major(rows, fsdp_size):
    count, width = rows.shape
    return rows.reshape(count, fsdp_size, 2, width // (2 * fsdp_size)).transpose(0, 2, 1, 3).reshape(
        count, width
    )


def reduce_weight_grad(grad):
    grad = lax.psum_scatter(grad.astype(jnp.bfloat16), "core", scatter_dimension=0, tiled=True)
    fsdp_size = lax.axis_size("fsdp")
    blocks = lax.all_to_all(
        grad.reshape((fsdp_size, -1) + grad.shape[1:]), "fsdp", split_axis=0, concat_axis=0, tiled=True
    )
    grad = jnp.sum(blocks.astype(jnp.float32), axis=0).astype(jnp.bfloat16)
    grad = lax.psum_scatter(grad, "zc", scatter_dimension=0, tiled=True)
    grad = lax.all_gather(grad, "zc", axis=0, tiled=True)
    grad = lax.all_gather(grad, "core", axis=0, tiled=True)
    return grad.astype(jnp.float32)


def shards(
    layer_in,
    out_grad,
    block_pairs,
    attn_gain,
    attn_shift,
    qkv_weight,
    query_bias,
    value_bias,
    out_weight,
    out_bias,
    mlp_gain,
    mlp_shift,
    fc_weight,
    fc_bias,
    proj_weight,
    proj_bias,
):
    fsdp_size = lax.axis_size("fsdp")
    ctx_size = lax.axis_size("zc") * lax.axis_size("core")
    seq_count = layer_in.shape[0]
    half_rows = layer_in.shape[3]
    model_width = layer_in.shape[4]
    block_len = half_rows * fsdp_size
    pair_len = 2 * block_len
    group_width = model_width // fsdp_size
    gathered = (
        gather_weight(qkv_weight),
        gather_weight(out_weight),
        gather_weight(fc_weight),
        gather_weight(proj_weight),
    )
    qkv_full, out_full, fc_full, proj_full = (gathered[0], gathered[1], gathered[2], gathered[3])
    vector_shards = (
        attn_gain,
        attn_shift,
        query_bias,
        value_bias,
        out_bias,
        mlp_gain,
        mlp_shift,
        fc_bias,
        proj_bias,
    )
    vector_pieces = lax.all_gather(jnp.concatenate(vector_shards), "fsdp", axis=0, tiled=False)
    vectors = []
    start = 0
    for shard in vector_shards:
        vectors.append(vector_pieces[:, start : start + shard.shape[0]].reshape(-1).astype(jnp.float32))
        start += shard.shape[0]
    (
        gain_attn,
        shift_attn,
        bias_query,
        bias_value,
        bias_out,
        gain_mlp,
        shift_mlp,
        bias_fc,
        bias_proj,
    ) = vectors
    halves = jnp.stack([block_pairs, 2 * ctx_size - 1 - block_pairs], axis=2)
    key_places = (halves[..., None] * block_len + jnp.arange(block_len, dtype=jnp.int32)).reshape(
        seq_count, ctx_size, pair_len
    )
    query_places = lax.dynamic_slice_in_dim(key_places, lax.axis_index(CTX), 1, 1).reshape(
        seq_count, pair_len
    )
    key_places = key_places.reshape(seq_count, ctx_size * pair_len)
    inputs = layer_in.reshape(-1, model_width).astype(jnp.float32)
    normed, attn_norm_back = jax.vjp(layer_norm, inputs, gain_attn, shift_attn)
    normed_low = normed.astype(jnp.bfloat16)
    mixed = jnp.dot(normed_low, qkv_full, preferred_element_type=jnp.float32)
    query = ((mixed[:, :model_width] + bias_query) * 0.125).astype(jnp.bfloat16)
    keys = mixed[:, model_width : 2 * model_width].astype(jnp.bfloat16)
    values = (mixed[:, 2 * model_width :] + bias_value).astype(jnp.bfloat16)

    def to_groups(array):
        return array.reshape(seq_count, 2, half_rows, fsdp_size, group_width)

    def to_pairs(array):
        return array.reshape(seq_count, 2, block_len, 1, group_width)

    qkv_heads = lax.all_to_all(
        jnp.concatenate([to_groups(query), to_groups(keys), to_groups(values)], axis=4),
        "fsdp",
        split_axis=3,
        concat_axis=2,
        tiled=True,
    ).reshape(seq_count, pair_len, 3 * group_width)
    query_heads = qkv_heads[..., :group_width]
    own_kv = qkv_heads[..., group_width:]
    kv_all = lax.all_gather(
        own_kv.reshape(seq_count, 1, pair_len, 2 * group_width), CTX, axis=1, tiled=True
    )
    key_all = kv_all[..., :group_width]
    value_all = kv_all[..., group_width:]
    key_all = key_all.reshape(seq_count, -1, group_width)
    value_all = value_all.reshape(seq_count, -1, group_width)
    attended, summary = lax.map(
        attend_forward, (query_heads, key_all, value_all, query_places, key_places)
    )
    attended_rows = lax.all_to_all(
        for_sending(to_pairs(attended)), "fsdp", split_axis=2, concat_axis=3, tiled=True
    ).reshape(-1, model_width)
    branch = jnp.dot(attended_rows, out_full, preferred_element_type=jnp.float32) + bias_out
    middle = inputs + branch
    normed_mlp, mlp_norm_back = jax.vjp(layer_norm, middle, gain_mlp, shift_mlp)
    mlp_low = normed_mlp.astype(jnp.bfloat16)
    hidden = jnp.dot(mlp_low, fc_full, preferred_element_type=jnp.float32) + bias_fc
    activated, gelu_back = jax.vjp(gelu_tanh, hidden)
    activated_low = activated.astype(jnp.bfloat16)
    result = (
        middle + jnp.dot(activated_low, proj_full, preferred_element_type=jnp.float32) + bias_proj
    )
    layer_out = result.astype(jnp.bfloat16).reshape(layer_in.shape)
    grad_rows = out_grad.reshape(-1, model_width)
    grad_result = grad_rows.astype(jnp.float32)
    proj_grad = contract_first(core_major(activated_low, fsdp_size), grad_rows)
    proj_bias_grad = jnp.sum(grad_result, axis=0)
    grad_activated = contract_last(grad_rows, proj_full)
    grad_hidden = gelu_back(grad_activated)[0].astype(jnp.bfloat16)
    fc_grad = contract_first(core_major(mlp_low, fsdp_size), grad_hidden)
    fc_bias_grad = jnp.sum(grad_hidden.astype(jnp.float32), axis=0)
    grad_middle, mlp_gain_grad, mlp_shift_grad = mlp_norm_back(contract_last(grad_hidden, fc_full))
    grad_middle = grad_middle + grad_result
    grad_branch = grad_middle.astype(jnp.bfloat16)
    out_weight_term = contract_first(core_major(attended_rows, fsdp_size), grad_branch)
    out_bias_grad = jnp.sum(grad_branch.astype(jnp.float32), axis=0)
    grad_attended = contract_last(grad_branch, out_full).astype(jnp.bfloat16)
    grad_heads = lax.all_to_all(
        to_groups(grad_attended), "fsdp", split_axis=3, concat_axis=2, tiled=True
    ).reshape(seq_count, pair_len, group_width)
    grad_query, grad_keys, grad_values = lax.map(
        attend_backward,
        (query_heads, key_all, value_all, grad_heads, summary, query_places, key_places),
    )
    kv_grads = jnp.concatenate([grad_keys, grad_values], axis=2).astype(jnp.bfloat16)
    kv_grads = kv_grads.reshape(seq_count, ctx_size, pair_len, 2 * group_width).transpose(1, 0, 2, 3)
    kv_part = lax.psum_scatter(
        kv_grads.reshape(ctx_size * seq_count * pair_len, 2 * group_width),
        CTX,
        scatter_dimension=0,
        tiled=True,
    ).reshape(seq_count, pair_len, 2 * group_width)
    key_part = kv_part[..., :group_width].astype(jnp.float32)
    value_part = kv_part[..., group_width:].astype(jnp.float32)
    key_grad_low = key_part.astype(jnp.bfloat16)
    value_grad_low = value_part.astype(jnp.bfloat16)
    query_back, key_back, value_back = (
        lax.all_to_all(
            for_sending(to_pairs(grad_query)), "fsdp", split_axis=2, concat_axis=3, tiled=True
        ),
        lax.all_to_all(
            for_sending(to_pairs(key_grad_low)), "fsdp", split_axis=2, concat_axis=3, tiled=True
        ),
        lax.all_to_all(
            for_sending(to_pairs(value_grad_low)), "fsdp", split_axis=2, concat_axis=3, tiled=True
        ),
    )
    grad_mixed = jnp.concatenate(
        [
            query_back.reshape(-1, model_width) * 0.125,
            key_back.reshape(-1, model_width),
            value_back.reshape(-1, model_width),
        ],
        axis=1,
    )
    qkv_grad = contract_first(core_major(normed_low, fsdp_size), grad_mixed)
    mixed_float = grad_mixed.astype(jnp.float32)
    query_bias_grad = jnp.sum(mixed_float[:, :model_width], axis=0)
    value_bias_grad = jnp.sum(mixed_float[:, 2 * model_width :], axis=0)
    grad_inputs, attn_gain_grad, attn_shift_grad = attn_norm_back(
        contract_last(grad_mixed, qkv_full)
    )
    in_grad = (grad_inputs + grad_middle).reshape(layer_in.shape)
    weight_totals = tuple(
        reduce_weight_grad(grad) for grad in (qkv_grad, out_weight_term, fc_grad, proj_grad)
    )
    vector_grads = (
        attn_gain_grad,
        attn_shift_grad,
        query_bias_grad,
        value_bias_grad,
        out_bias_grad,
        mlp_gain_grad,
        mlp_shift_grad,
        fc_bias_grad,
        proj_bias_grad,
    )
    packed = jnp.concatenate([grad.reshape(fsdp_size, -1) for grad in vector_grads], axis=1)
    packed = lax.psum(packed.astype(jnp.float32), CTX + ("fsdp",))
    packed = lax.dynamic_index_in_dim(packed, lax.axis_index("fsdp"), 0, keepdims=False)
    vector_totals = []
    offset = 0
    for grad in vector_grads:
        width = grad.shape[0] // fsdp_size
        vector_totals.append(packed[offset : offset + width])
        offset += width
    totals = weight_totals + tuple(vector_totals)
    return (
        layer_out,
        in_grad,
        totals[4],
        totals[5],
        totals[0],
        totals[6],
        totals[7],
        totals[1],
        totals[8],
        totals[9],
        totals[10],
        totals[2],
        totals[11],
        totals[3],
        totals[12],
    )


def solution(mesh):
    ctx_count, fsdp_count = mesh.devices.shape
    mesh = jax.sharding.Mesh(
        mesh.devices.reshape(ctx_count // 2, 2, fsdp_count), ("zc", "core", "fsdp")
    )
    placed = (
        P(None, CTX, None, "fsdp", None),
        P(None, CTX, None, "fsdp", None),
        P(),
        P("fsdp"),
        P("fsdp"),
        P("fsdp", None),
        P("fsdp"),
        P("fsdp"),
        P("fsdp", None),
        P("fsdp"),
        P("fsdp"),
        P("fsdp"),
        P("fsdp", None),
        P("fsdp"),
        P("fsdp", None),
        P("fsdp"),
    )
    return jax.shard_map(
        shards,
        mesh=mesh,
        in_specs=placed,
        out_specs=(
            P(None, CTX, None, "fsdp", None),
            P(None, CTX, None, "fsdp", None),
            P("fsdp"),
            P("fsdp"),
            P("fsdp", None),
            P("fsdp"),
            P("fsdp"),
            P("fsdp", None),
            P("fsdp"),
            P("fsdp"),
            P("fsdp"),
            P("fsdp", None),
            P("fsdp"),
            P("fsdp", None),
            P("fsdp"),
        ),
        check_vma=False,
    )
```
